768 devices in a mesh: tile: 64 (over z_hi, y, core), sec: 3 (over z_lo), ch: 4 (over x).
Axes of the slice: x: 4, y: 8, z: 12 (z_hi: 4, z_lo: 3; z = z_hi * 3 + z_lo), core: 2. Of those that a mesh axis runs over, the one named last changes fastest.
Arguments:
- fields: bfloat16 [64, 64, 1024], P('ch', 'tile'), may hold values from -6 to 6
- cotangent: bfloat16 [64, 64, 1024], P('ch', 'tile'), may hold values from -6 to 6
- depth_kernel: float32 [3, 64, 9], P('sec', 'ch'), may hold values from -2 to 2
- norm_gain: float32 [3, 64], P('sec'), may hold values from 0.5 to 1.5
- up_weight: bfloat16 [3, 64, 256], P('sec'), may hold values from -0.75 to 0.75
- down_weight: bfloat16 [3, 256, 64], P('sec'), may hold values from -0.375 to 0.375
- layer_scale: float32 [3, 64], P('sec', 'ch'), may hold values from 0.3 to 1.5
- skip_scale: float32 [64], P('ch'), may hold values from 0.3 to 1.5
- neighbours: int32 [64, 4], replicated, may hold values from 0 to 63, as said below
- edge_codes: int32 [64, 4], replicated, may hold values from 0 to 7, as said below
- offsets: int32 [64], P('tile'), may hold values from 0 to 64512, as said below
- drop_seed: int32 [1], replicated, may hold values from 0 to 999999
Outputs:
- section_outputs: bfloat16 [3, 64, 64, 1024], P('sec', 'ch', 'tile')
- input_grads: float32 [3, 64, 64, 1024], P('sec', 'ch', 'tile')
The draws below stay inside these ranges and needn't reach their ends.
Inputs may be any that keep to these rules, and one draw needn't show every extreme that they name: Side e of tile t meets side edge_codes[t, e] % 4 of tile neighbours[t, e]; the sides form a matching: if side e of t meets side e2 of t2, side e2 of t2 meets side e of t. Both sides of a meeting carry the same reversal, edge_codes // 4. `offsets`: multiples of 1024; the tiles' pixel ranges cover 0 to 65535 once.
All inputs are finite; a program needn't handle non-finite values.
Results may differ from the reference program's by a relative error of at most 0.0065.
Values may be sent and summed in bfloat16 or wider, within the bound.
No kernel may reach another device: no remote copies, remote signals or barrier semaphores. Data moves between devices by JAX's collectives and lax.ppermute only.
A program may use at most 32 MiB of HBM per device.

```python
import math
import jax
import jax.numpy as jnp
from jax import lax

C = 64
UNITS = 256
SIDE = 32
AREA = 1024
TILES = 64
N_SEC = 3


def edge_matching(key):
    slot_count = TILES * 4
    shuffled = jax.random.permutation(jax.random.fold_in(key, 11), slot_count).astype(jnp.int32)
    first_half = shuffled[0::2]
    second_half = shuffled[1::2]
    partner = jnp.zeros((slot_count,), jnp.int32).at[first_half].set(second_half).at[second_half].set(first_half)
    turned = jax.random.randint(jax.random.fold_in(key, 12), (slot_count // 2,), 0, 2, dtype=jnp.int32)
    reverse_bit = jnp.zeros((slot_count,), jnp.int32).at[first_half].set(turned).at[second_half].set(turned)
    return (partner, reverse_bit)


def draw_neighbours(key, part):
    partner, reverse_bit = edge_matching(key)
    return (partner // 4).reshape(TILES, 4)


def draw_edge_codes(key, part):
    partner, reverse_bit = edge_matching(key)
    return (partner % 4 + 4 * reverse_bit).reshape(TILES, 4)


def draw_offsets(key, part):
    shuffled = jax.random.permutation(jax.random.fold_in(key, 13), TILES).astype(jnp.int32)
    return (shuffled * AREA).astype(jnp.int32)


def steps_of(own_key, dims, split, low, high):
    gain = 1.0
    for axis_at, blocks in split:
        steps = jax.random.uniform(jax.random.fold_in(jax.random.fold_in(own_key, 6), axis_at), (blocks,), jnp.float32, low / len(split), high / len(split))
        gain = gain * jnp.repeat(jnp.exp(steps), dims[axis_at] // blocks).reshape((-1,) + (1,) * (len(dims) - 1 - axis_at))
    return gain


def bell_draw(own_key, dims, width, reach, shards=(), kind=jnp.bfloat16):
    gain = steps_of(own_key, dims, shards, -0.22, 0.18) if shards else 1.0
    result = jax.random.normal(own_key, dims, jnp.float32) * width * gain
    return jnp.minimum(jnp.maximum(result, -reach), reach).astype(kind)


def setup_inputs(seed: int = 0) -> dict:
    keys = jax.random.split(jax.random.key(seed), 13)
    fields = bell_draw(keys[0], (C, TILES, AREA), 1.0, 6.0, ((0, 4), (1, 64)))
    cotangent = bell_draw(keys[1], (C, TILES, AREA), 1.0, 6.0, ((0, 4), (1, 64)))
    depth_kernel = bell_draw(keys[2], (N_SEC, C, 9), 9 ** -0.5, 2.0, ((0, 3), (1, 4)), jnp.float32)
    norm_gain = jnp.clip(1.0 + 0.1 * jax.random.normal(keys[3], (N_SEC, C), jnp.float32), 0.5, 1.5)
    up_weight = bell_draw(keys[4], (N_SEC, C, UNITS), C ** -0.5, 0.75, ((0, 3),))
    down_weight = bell_draw(keys[5], (N_SEC, UNITS, C), UNITS ** -0.5, 0.375, ((0, 3),))
    layer_scale = jnp.clip(jnp.exp(math.log(1.5) - 1.60943787 * jax.random.uniform(keys[6], (N_SEC, C), jnp.float32) ** steps_of(keys[6], (N_SEC, C), ((0, 3), (1, 4)), -0.2, 0.2)), 0.3, 1.5)
    skip_scale = jnp.clip(jnp.exp(math.log(1.5) - 1.60943787 * jax.random.uniform(keys[7], (C,), jnp.float32) ** steps_of(keys[7], (C,), ((0, 4),), -0.2, 0.2)), 0.3, 1.5)
    neighbours = draw_neighbours(jax.random.fold_in(keys[12], 71), 0)
    edge_codes = draw_edge_codes(jax.random.fold_in(keys[12], 71), 0)
    offsets = draw_offsets(jax.random.fold_in(keys[12], 71), 0)
    drop_seed = jax.random.randint(keys[11], (1,), 0, 1000000).astype(jnp.int32)
    return dict(fields=fields, cotangent=cotangent, depth_kernel=depth_kernel, norm_gain=norm_gain, up_weight=up_weight, down_weight=down_weight, layer_scale=layer_scale, skip_scale=skip_scale, neighbours=neighbours, edge_codes=edge_codes, offsets=offsets, drop_seed=drop_seed)


drop_scale = 1.0 / 0.9
gelu_coeff = 0.7978845608028654
cubic_coeff = 0.044715

def mix_bits(counter):
    counter = counter * jnp.int32(739982445)
    counter = counter ^ lax.shift_right_logical(counter, jnp.int32(15))
    counter = counter * jnp.int32(695872825)
    counter = counter ^ lax.shift_right_logical(counter, jnp.int32(12))
    return counter

def keep_mask(drop_seed, section, unit_ids, pixels, hidden):
    salted = mix_bits(drop_seed + section * jnp.int32(1000003))
    counter = pixels[None, :] * jnp.int32(hidden) + unit_ids[:, None]
    mixed_bits = mix_bits(counter ^ salted)
    return (mixed_bits & jnp.int32(65535) >= jnp.int32(6554)).astype(jnp.float32)

def layer_norm(columns, norm_gain):
    centre = columns - lax.optimization_barrier(jnp.mean(columns, axis=0, keepdims=True))
    inverse_dev = lax.rsqrt(lax.optimization_barrier(jnp.mean(centre * centre, axis=0, keepdims=True)) + 1e-06)
    normed = centre * inverse_dev
    return (normed, inverse_dev, (normed * norm_gain[:, None]).astype(jnp.bfloat16))

def norm_back(grad_in, normed, inverse_dev, norm_gain):
    scaled = grad_in * norm_gain[:, None]
    return inverse_dev * (scaled - lax.optimization_barrier(jnp.mean(scaled, axis=0, keepdims=True)) - normed * lax.optimization_barrier(jnp.mean(scaled * normed, axis=0, keepdims=True)))

def gelu_value(pre_act):
    tanh_part = jnp.tanh(gelu_coeff * (pre_act + cubic_coeff * pre_act * pre_act * pre_act))
    return 0.5 * pre_act * (1.0 + tanh_part)

def gelu_slope(pre_act):
    tanh_part = jnp.tanh(gelu_coeff * (pre_act + cubic_coeff * pre_act * pre_act * pre_act))
    return 0.5 * (1.0 + tanh_part) + 0.5 * pre_act * (1.0 - tanh_part * tanh_part) * gelu_coeff * (1.0 + 3.0 * cubic_coeff * pre_act * pre_act)

def border_lines(tile_grid):
    return jnp.stack([tile_grid[:, :, 0, :], tile_grid[:, :, -1, :], tile_grid[:, :, :, 0], tile_grid[:, :, :, -1]], axis=2)

def pad_tiles(tile_grid, halo_rows):
    zero_corner = jnp.zeros(tile_grid.shape[:2] + (1, 1), tile_grid.dtype)
    middle = jnp.concatenate([halo_rows[:, :, 2, :, None], tile_grid, halo_rows[:, :, 3, :, None]], axis=3)
    top_row = jnp.concatenate([zero_corner, halo_rows[:, :, 0, None, :], zero_corner], axis=3)
    bottom_row = jnp.concatenate([zero_corner, halo_rows[:, :, 1, None, :], zero_corner], axis=3)
    return jnp.concatenate([top_row, middle, bottom_row], axis=2)

def depthwise(padded, depth_kernel):
    side_len = padded.shape[2] - 2
    running = jnp.zeros(padded.shape[:2] + (side_len, side_len), jnp.float32)
    for down_step in range(3):
        for right_step in range(3):
            weight_now = depth_kernel[:, down_step * 3 + right_step][:, None, None, None]
            running = running + weight_now * padded[:, :, down_step:down_step + side_len, right_step:right_step + side_len].astype(jnp.float32)
    return running

def depth_back(grad_in, depth_kernel):
    side_len = grad_in.shape[2]
    widened = jnp.pad(grad_in, ((0, 0), (0, 0), (2, 2), (2, 2)))
    running = jnp.zeros(grad_in.shape[:2] + (side_len + 2, side_len + 2), jnp.float32)
    for down_step in range(3):
        for right_step in range(3):
            weight_now = depth_kernel[:, down_step * 3 + right_step][:, None, None, None]
            running = running + weight_now * widened[:, :, 2 - down_step:4 - down_step + side_len, 2 - right_step:4 - right_step + side_len]
    return running

def halo_parts(padded):
    return jnp.stack([padded[:, :, 0, 1:-1], padded[:, :, -1, 1:-1], padded[:, :, 1:-1, 0], padded[:, :, 1:-1, -1]], axis=2)

def add_border(interior, border):
    interior = interior.at[:, :, 0, :].add(border[:, :, 0])
    interior = interior.at[:, :, -1, :].add(border[:, :, 1])
    interior = interior.at[:, :, :, 0].add(border[:, :, 2])
    return interior.at[:, :, :, -1].add(border[:, :, 3])

def block_forward(block_in, section, weights, source, flipped, offsets, drop_seed):
    depth_kernel, norm_gain, up_weight, down_weight, layer_scale = weights
    chan_count, tile_count, tile_area = block_in.shape
    tile_grid = block_in.reshape(chan_count, tile_count, SIDE, SIDE)
    edge_rows = border_lines(tile_grid).reshape(chan_count, tile_count * 4, SIDE)
    halo_rows = jnp.take(edge_rows, source.reshape(-1), axis=1).reshape(chan_count, tile_count, 4, SIDE)
    halo_rows = jnp.where(flipped[None, :, :, None], halo_rows[..., ::-1], halo_rows)
    mixed_in = depthwise(pad_tiles(tile_grid, halo_rows), depth_kernel).astype(jnp.bfloat16).reshape(chan_count, -1)
    normed, inverse_dev, scaled_in = layer_norm(mixed_in.astype(jnp.float32), norm_gain)
    hidden = up_weight.shape[1]
    pre_act = jnp.dot(up_weight.T, scaled_in, preferred_element_type=jnp.float32)
    pixels = (offsets[:, None] + jnp.arange(tile_area, dtype=jnp.int32)[None, :]).reshape(-1)
    keeper = keep_mask(drop_seed, section, jnp.arange(hidden, dtype=jnp.int32), pixels, hidden)
    dropped = (gelu_value(pre_act) * keeper * drop_scale).astype(jnp.bfloat16)
    branch = jnp.dot(down_weight.T, dropped, preferred_element_type=jnp.float32)
    output = (block_in.astype(jnp.float32) + layer_scale[:, None, None] * branch.reshape(chan_count, tile_count, tile_area)).astype(jnp.bfloat16)
    return (output, (normed, inverse_dev, pre_act, keeper))

def block_backward(grad_out, weights, stored, source, flipped):
    depth_kernel, norm_gain, up_weight, down_weight, layer_scale = weights
    normed, inverse_dev, pre_act, keeper = stored
    chan_count, tile_count, tile_area = grad_out.shape
    scaled_grad = (layer_scale[:, None, None] * grad_out).astype(jnp.bfloat16).reshape(chan_count, -1)
    grad_drop = jnp.dot(down_weight, scaled_grad, preferred_element_type=jnp.float32)
    grad_pre = (grad_drop * keeper * drop_scale * gelu_slope(pre_act)).astype(jnp.bfloat16)
    grad_norm = jnp.dot(up_weight, grad_pre, preferred_element_type=jnp.float32)
    grad_mixed = norm_back(grad_norm, normed, inverse_dev, norm_gain)
    grad_padded = depth_back(grad_mixed.reshape(chan_count, tile_count, SIDE, SIDE), depth_kernel)
    edge_grad = halo_parts(grad_padded)
    edge_grad = jnp.where(flipped[None, :, :, None], edge_grad[..., ::-1], edge_grad).astype(jnp.bfloat16)
    slot_major = jnp.moveaxis(edge_grad.reshape(chan_count, tile_count * 4, SIDE), 1, 0).astype(jnp.float32)
    routed = jax.ops.segment_sum(slot_major, source.reshape(-1), num_segments=tile_count * 4)
    routed = jnp.moveaxis(routed, 0, 1).reshape(chan_count, tile_count, 4, SIDE)
    interior = add_border(grad_padded[:, :, 1:-1, 1:-1], routed)
    return grad_out + interior.reshape(chan_count, tile_count, tile_area)

def reference(fields, cotangent, depth_kernel, norm_gain, up_weight, down_weight, layer_scale, skip_scale, neighbours, edge_codes, offsets, drop_seed):
    source = neighbours * 4 + edge_codes % 4
    flipped = edge_codes >= 4
    sections = depth_kernel.shape[0]
    out_list = []
    stored_list = []
    current = fields
    encoded = fields
    for section in range(sections):
        if section == sections - 1:
            current = (current.astype(jnp.float32) + skip_scale[:, None, None] * encoded.astype(jnp.float32)).astype(jnp.bfloat16)
        weights = (depth_kernel[section], norm_gain[section], up_weight[section], down_weight[section], layer_scale[section])
        output, stored = block_forward(current, section, weights, source, flipped, offsets, drop_seed)
        if section == 0:
            encoded = output
        out_list.append(output)
        stored_list.append(stored)
        current = output
    grad_list = [None] * sections
    grad_now = cotangent.astype(jnp.float32)
    skip_grad = jnp.zeros_like(grad_now)
    for section in reversed(range(sections)):
        if section == 0:
            grad_now = grad_now + skip_grad
        weights = (depth_kernel[section], norm_gain[section], up_weight[section], down_weight[section], layer_scale[section])
        grad_in = block_backward(grad_now, weights, stored_list[section], source, flipped)
        grad_list[section] = grad_in
        if section == sections - 1:
            skip_grad = skip_scale[:, None, None] * grad_in
        grad_now = grad_in
    return (jnp.stack(out_list), jnp.stack(grad_list))
```

```python
import jax
import jax.numpy as jnp
from jax import lax
from jax.sharding import PartitionSpec as P

SIDE = 32


drop_scale = 1.0 / 0.9
gelu_coeff = 0.7978845608028654
cubic_coeff = 0.044715


def mix_bits(counter):
    counter = counter * jnp.int32(739982445)
    counter = counter ^ lax.shift_right_logical(counter, jnp.int32(15))
    counter = counter * jnp.int32(695872825)
    counter = counter ^ lax.shift_right_logical(counter, jnp.int32(12))
    return counter


def keep_mask(drop_seed, section, unit_ids, pixels, hidden):
    salted = mix_bits(drop_seed + section * jnp.int32(1000003))
    counter = pixels[None, :] * jnp.int32(hidden) + unit_ids[:, None]
    mixed_bits = mix_bits(counter ^ salted)
    return (mixed_bits & jnp.int32(65535) >= jnp.int32(6554)).astype(jnp.float32)


def layer_norm(columns, norm_gain):
    centre = columns - jnp.mean(columns, axis=0, keepdims=True)
    inverse_dev = lax.rsqrt(jnp.mean(centre * centre, axis=0, keepdims=True) + 1e-06)
    normed = centre * inverse_dev
    return (normed, inverse_dev, (normed * norm_gain[:, None]).astype(jnp.bfloat16))


def norm_back(grad_in, normed, inverse_dev, norm_gain):
    scaled = grad_in * norm_gain[:, None]
    return inverse_dev * (
        scaled
        - jnp.mean(scaled, axis=0, keepdims=True)
        - normed * jnp.mean(scaled * normed, axis=0, keepdims=True)
    )


def gelu_value(pre_act):
    tanh_part = jnp.tanh(gelu_coeff * (pre_act + cubic_coeff * pre_act * pre_act * pre_act))
    return 0.5 * pre_act * (1.0 + tanh_part)


def gelu_slope(pre_act):
    tanh_part = jnp.tanh(gelu_coeff * (pre_act + cubic_coeff * pre_act * pre_act * pre_act))
    return 0.5 * (1.0 + tanh_part) + 0.5 * pre_act * (1.0 - tanh_part * tanh_part) * gelu_coeff * (
        1.0 + 3.0 * cubic_coeff * pre_act * pre_act
    )


def border_lines(grid):
    return jnp.stack([grid[:, 0, :], grid[:, -1, :], grid[:, :, 0], grid[:, :, -1]], axis=0)


def pad_tile(grid, halo):
    zero_corner = jnp.zeros(grid.shape[:1] + (1, 1), grid.dtype)
    middle = jnp.concatenate([halo[2][:, :, None], grid, halo[3][:, :, None]], axis=2)
    top_row = jnp.concatenate([zero_corner, halo[0][:, None, :], zero_corner], axis=2)
    bottom_row = jnp.concatenate([zero_corner, halo[1][:, None, :], zero_corner], axis=2)
    return jnp.concatenate([top_row, middle, bottom_row], axis=1)


def depthwise(padded, depth_kernel):
    side_len = padded.shape[1] - 2
    running = jnp.zeros(padded.shape[:1] + (side_len, side_len), jnp.float32)
    for down_step in range(3):
        for right_step in range(3):
            weight_now = depth_kernel[:, down_step * 3 + right_step][:, None, None]
            running = running + weight_now * padded[
                :, down_step : down_step + side_len, right_step : right_step + side_len
            ].astype(jnp.float32)
    return running


def depth_back(grad_in, depth_kernel):
    side_len = grad_in.shape[1]
    widened = jnp.pad(grad_in, ((0, 0), (2, 2), (2, 2)))
    running = jnp.zeros(grad_in.shape[:1] + (side_len + 2, side_len + 2), jnp.float32)
    for down_step in range(3):
        for right_step in range(3):
            weight_now = depth_kernel[:, down_step * 3 + right_step][:, None, None]
            running = running + weight_now * widened[
                :,
                2 - down_step : 4 - down_step + side_len,
                2 - right_step : 4 - right_step + side_len,
            ]
    return running


def halo_parts(padded):
    return jnp.stack(
        [padded[:, 0, 1:-1], padded[:, -1, 1:-1], padded[:, 1:-1, 0], padded[:, 1:-1, -1]], axis=0
    )


def add_border(interior, border):
    interior = interior.at[:, 0, :].add(border[0])
    interior = interior.at[:, -1, :].add(border[1])
    interior = interior.at[:, :, 0].add(border[2])
    return interior.at[:, :, -1].add(border[3])


def shards(
    fields,
    cotangent,
    depth_kernel,
    norm_gain,
    up_weight,
    down_weight,
    layer_scale,
    skip_scale,
    neighbours,
    edge_codes,
    offsets,
    drop_seed,
):
    chan_part, tile_dev, tile_area = fields.shape
    assert tile_dev == 1
    side_len = SIDE
    my_phase = lax.axis_index("sec")
    sections = lax.axis_size("sec")
    ch_index = lax.axis_index("ch")
    ch_count = lax.axis_size("ch")
    tile_count = lax.axis_size("tile")
    my_tile = lax.axis_index("tile")
    hidden = up_weight.shape[2]
    pix_part = tile_area // ch_count

    dk_all = lax.all_gather(depth_kernel, "sec", axis=0, tiled=True)
    gain_all = lax.all_gather(norm_gain, "sec", axis=0, tiled=True)
    up_all = lax.all_gather(up_weight, "sec", axis=0, tiled=True)
    down_all = lax.all_gather(down_weight, "sec", axis=0, tiled=True)
    scale_all = lax.all_gather(layer_scale, "sec", axis=0, tiled=True)

    side_code = edge_codes % 4
    own_flip = edge_codes[my_tile] >= 4
    fwd_pick = (
        (neighbours[:, :, None] == my_tile)
        & (side_code[:, :, None] == jnp.arange(4, dtype=jnp.int32)[None, None, :])
    ).astype(jnp.bfloat16)
    own_nb = neighbours[my_tile]
    own_code = side_code[my_tile]
    bwd_pick = (
        (own_nb[None, None, :] == jnp.arange(tile_count, dtype=jnp.int32)[:, None, None])
        & (own_code[None, None, :] == jnp.arange(4, dtype=jnp.int32)[None, :, None])
    ).astype(jnp.bfloat16)

    pixel_ids = offsets[0] + ch_index * pix_part + jnp.arange(pix_part, dtype=jnp.int32)
    unit_ids = jnp.arange(hidden, dtype=jnp.int32)

    def route(lines, pick):
        send = jnp.einsum("jek,kcs->jecs", pick, lines, preferred_element_type=jnp.float32)
        send = send.astype(jnp.bfloat16).reshape(tile_count, -1)
        got = lax.all_to_all(send, "tile", 0, 0, tiled=True)
        got = got.reshape(tile_count, 4, chan_part, side_len).astype(jnp.float32)
        return jnp.sum(got, axis=0)

    def to_pixels(block):
        return lax.all_to_all(block, "ch", 1, 0, tiled=True)

    def to_channels(block):
        return lax.all_to_all(block, "ch", 0, 1, tiled=True)

    def block_forward(block_in, s):
        grid = block_in.reshape(chan_part, side_len, side_len)
        halo = route(border_lines(grid), fwd_pick).astype(jnp.bfloat16)
        halo = jnp.where(own_flip[:, None, None], halo[..., ::-1], halo)
        mixed = depthwise(pad_tile(grid, halo), dk_all[s]).astype(jnp.bfloat16)
        cols = to_pixels(mixed.reshape(chan_part, tile_area))
        normed, inverse_dev, scaled_in = layer_norm(cols.astype(jnp.float32), gain_all[s])
        pre_act = jnp.einsum("ch,cp->hp", up_all[s], scaled_in, preferred_element_type=jnp.float32)
        keeper = keep_mask(drop_seed, s, unit_ids, pixel_ids, hidden)
        dropped = (gelu_value(pre_act) * keeper * drop_scale).astype(jnp.bfloat16)
        branch = jnp.einsum("hc,hp->cp", down_all[s], dropped, preferred_element_type=jnp.float32)
        branch = to_channels(branch)
        out = (
            block_in.astype(jnp.float32) + scale_all[s][:, None] * branch
        ).astype(jnp.bfloat16)
        return out, (normed, inverse_dev, pre_act, keeper)

    def block_backward(grad_out, stored, s):
        normed, inverse_dev, pre_act, keeper = stored
        scaled_grad = (scale_all[s][:, None] * grad_out).astype(jnp.bfloat16)
        cols = to_pixels(scaled_grad)
        grad_drop = jnp.einsum("hc,cp->hp", down_all[s], cols, preferred_element_type=jnp.float32)
        grad_pre = (grad_drop * keeper * drop_scale * gelu_slope(pre_act)).astype(jnp.bfloat16)
        grad_norm = jnp.einsum("ch,hp->cp", up_all[s], grad_pre, preferred_element_type=jnp.float32)
        grad_mixed = norm_back(grad_norm, normed, inverse_dev, gain_all[s])
        grad_mixed = to_channels(grad_mixed).reshape(chan_part, side_len, side_len)
        grad_padded = depth_back(grad_mixed, dk_all[s])
        edge_grad = halo_parts(grad_padded)
        edge_grad = jnp.where(own_flip[:, None, None], edge_grad[..., ::-1], edge_grad).astype(
            jnp.bfloat16
        )
        routed = route(edge_grad, bwd_pick)
        interior = add_border(grad_padded[:, 1:-1, 1:-1], routed)
        return grad_out + interior.reshape(chan_part, tile_area)

    skip_col = skip_scale[:, None]
    current = fields.reshape(chan_part, tile_area)
    outs = []
    stores = []
    for s in range(sections):
        if s == sections - 1:
            current = (
                current.astype(jnp.float32) + skip_col * outs[0].astype(jnp.float32)
            ).astype(jnp.bfloat16)
        current, stored = block_forward(current, s)
        outs.append(current)
        stores.append(stored)
    grads = [None] * sections
    grad_now = cotangent.reshape(chan_part, tile_area).astype(jnp.float32)
    skip_grad = None
    for s in reversed(range(sections)):
        if s == 0 and sections > 1:
            grad_now = grad_now + skip_grad
        grad_now = block_backward(grad_now, stores[s], s)
        grads[s] = grad_now
        if s == sections - 1:
            skip_grad = skip_col * grad_now
    act_keep = outs[0]
    grad_keep = grads[0]
    for s in range(1, sections):
        act_keep = jnp.where(my_phase == s, outs[s], act_keep)
        grad_keep = jnp.where(my_phase == s, grads[s], grad_keep)
    return (
        act_keep.reshape(1, chan_part, tile_dev, tile_area),
        grad_keep.reshape(1, chan_part, tile_dev, tile_area),
    )


def solution(mesh):
    placed = (
        P("ch", "tile", None),
        P("ch", "tile", None),
        P("sec", "ch", None),
        P("sec", None),
        P("sec", None, None),
        P("sec", None, None),
        P("sec", "ch"),
        P("ch"),
        P(),
        P(),
        P("tile"),
        P(),
    )
    return jax.shard_map(
        shards,
        mesh=mesh,
        in_specs=placed,
        out_specs=(P("sec", "ch", "tile", None), P("sec", "ch", "tile", None)),
        check_vma=False,
    )
```

```python
import jax
import jax.numpy as jnp
from jax import lax
from jax.sharding import PartitionSpec as P

SIDE = 32


drop_scale = 1.0 / 0.9
gelu_coeff = 0.7978845608028654
cubic_coeff = 0.044715


def mix_bits(counter):
    counter = counter * jnp.int32(739982445)
    counter = counter ^ lax.shift_right_logical(counter, jnp.int32(15))
    counter = counter * jnp.int32(695872825)
    counter = counter ^ lax.shift_right_logical(counter, jnp.int32(12))
    return counter


def keep_mask(drop_seed, section, unit_ids, pixels, hidden):
    salted = mix_bits(drop_seed + section * jnp.int32(1000003))
    counter = pixels[None, :] * jnp.int32(hidden) + unit_ids[:, None]
    mixed_bits = mix_bits(counter ^ salted)
    return (mixed_bits & jnp.int32(65535) >= jnp.int32(6554)).astype(jnp.float32)


def layer_norm(columns, norm_gain):
    centre = columns - jnp.mean(columns, axis=0, keepdims=True)
    inverse_dev = lax.rsqrt(jnp.mean(centre * centre, axis=0, keepdims=True) + 1e-06)
    normed = centre * inverse_dev
    return (normed, inverse_dev, (normed * norm_gain[:, None]).astype(jnp.bfloat16))


def norm_back(grad_in, normed, inverse_dev, norm_gain):
    scaled = grad_in * norm_gain[:, None]
    return inverse_dev * (
        scaled
        - jnp.mean(scaled, axis=0, keepdims=True)
        - normed * jnp.mean(scaled * normed, axis=0, keepdims=True)
    )


def gelu_value(pre_act):
    tanh_part = jnp.tanh(gelu_coeff * (pre_act + cubic_coeff * pre_act * pre_act * pre_act))
    return 0.5 * pre_act * (1.0 + tanh_part)


def gelu_slope(pre_act):
    tanh_part = jnp.tanh(gelu_coeff * (pre_act + cubic_coeff * pre_act * pre_act * pre_act))
    return 0.5 * (1.0 + tanh_part) + 0.5 * pre_act * (1.0 - tanh_part * tanh_part) * gelu_coeff * (
        1.0 + 3.0 * cubic_coeff * pre_act * pre_act
    )


def border_lines(grid):
    return jnp.stack([grid[:, 0, :], grid[:, -1, :], grid[:, :, 0], grid[:, :, -1]], axis=0)


def pad_tile(grid, halo):
    zero_corner = jnp.zeros(grid.shape[:1] + (1, 1), grid.dtype)
    middle = jnp.concatenate([halo[2][:, :, None], grid, halo[3][:, :, None]], axis=2)
    top_row = jnp.concatenate([zero_corner, halo[0][:, None, :], zero_corner], axis=2)
    bottom_row = jnp.concatenate([zero_corner, halo[1][:, None, :], zero_corner], axis=2)
    return jnp.concatenate([top_row, middle, bottom_row], axis=1)


def depthwise(padded, depth_kernel):
    side_len = padded.shape[1] - 2
    running = jnp.zeros(padded.shape[:1] + (side_len, side_len), jnp.float32)
    for down_step in range(3):
        for right_step in range(3):
            weight_now = depth_kernel[:, down_step * 3 + right_step][:, None, None]
            running = running + weight_now * padded[
                :, down_step : down_step + side_len, right_step : right_step + side_len
            ].astype(jnp.float32)
    return running


def depth_back(grad_in, depth_kernel):
    side_len = grad_in.shape[1]
    widened = jnp.pad(grad_in, ((0, 0), (2, 2), (2, 2)))
    running = jnp.zeros(grad_in.shape[:1] + (side_len + 2, side_len + 2), jnp.float32)
    for down_step in range(3):
        for right_step in range(3):
            weight_now = depth_kernel[:, down_step * 3 + right_step][:, None, None]
            running = running + weight_now * widened[
                :,
                2 - down_step : 4 - down_step + side_len,
                2 - right_step : 4 - right_step + side_len,
            ]
    return running


def halo_parts(padded):
    return jnp.stack(
        [padded[:, 0, 1:-1], padded[:, -1, 1:-1], padded[:, 1:-1, 0], padded[:, 1:-1, -1]], axis=0
    )


def add_border(interior, border):
    interior = interior.at[:, 0, :].add(border[0])
    interior = interior.at[:, -1, :].add(border[1])
    interior = interior.at[:, :, 0].add(border[2])
    return interior.at[:, :, -1].add(border[3])


def shards(
    fields,
    cotangent,
    depth_kernel,
    norm_gain,
    up_weight,
    down_weight,
    layer_scale,
    skip_scale,
    neighbours,
    edge_codes,
    offsets,
    drop_seed,
):
    chan_part, tile_dev, tile_area = fields.shape
    assert tile_dev == 1
    side_len = SIDE
    my_phase = lax.axis_index("sec")
    sections = lax.axis_size("sec")
    ch_index = lax.axis_index("ch")
    ch_count = lax.axis_size("ch")
    tile_count = lax.axis_size("tile")
    my_tile = lax.axis_index("tile")
    hidden = up_weight.shape[2]
    pix_part = tile_area // ch_count

    small = jnp.concatenate(
        [depth_kernel[0].reshape(-1), norm_gain[0], layer_scale[0]]
    )
    large = jnp.concatenate([up_weight[0].reshape(-1), down_weight[0].reshape(-1)])
    small_got = [small]
    large_got = [large]
    for shift in range(1, sections):
        route_now = [(i, (i + shift) % sections) for i in range(sections)]
        small_got.append(lax.ppermute(small, "sec", route_now))
        large_got.append(lax.ppermute(large, "sec", route_now))

    def section_weights(s):
        behind = (my_phase - s) % sections
        small_s = small_got[0]
        large_s = large_got[0]
        for shift in range(1, sections):
            small_s = jnp.where(behind == shift, small_got[shift], small_s)
            large_s = jnp.where(behind == shift, large_got[shift], large_s)
        dk_len = chan_part * 9
        cut = up_weight.shape[1] * hidden
        return (
            small_s[:dk_len].reshape(chan_part, 9),
            small_s[dk_len : dk_len + norm_gain.shape[1]],
            small_s[dk_len + norm_gain.shape[1] :],
            large_s[:cut].reshape(up_weight.shape[1:]),
            large_s[cut:].reshape(down_weight.shape[1:]),
        )

    weights = [section_weights(s) for s in range(sections)]
    dk_all = [w[0] for w in weights]
    gain_all = [w[1] for w in weights]
    scale_all = [w[2] for w in weights]
    up_all = [w[3] for w in weights]
    down_all = [w[4] for w in weights]

    side_code = edge_codes % 4
    own_flip = edge_codes[my_tile] >= 4
    fwd_pick = (
        (neighbours[:, :, None] == my_tile)
        & (side_code[:, :, None] == jnp.arange(4, dtype=jnp.int32)[None, None, :])
    ).astype(jnp.bfloat16)
    own_nb = neighbours[my_tile]
    own_code = side_code[my_tile]
    bwd_pick = (
        (own_nb[None, None, :] == jnp.arange(tile_count, dtype=jnp.int32)[:, None, None])
        & (own_code[None, None, :] == jnp.arange(4, dtype=jnp.int32)[None, :, None])
    ).astype(jnp.bfloat16)

    pixel_ids = offsets[0] + ch_index * pix_part + jnp.arange(pix_part, dtype=jnp.int32)
    unit_ids = jnp.arange(hidden, dtype=jnp.int32)

    def route(lines, pick):
        send = jnp.einsum("jek,kcs->jecs", pick, lines, preferred_element_type=jnp.float32)
        send = send.astype(jnp.bfloat16).reshape(tile_count, -1)
        got = lax.all_to_all(send, "tile", 0, 0, tiled=True)
        got = got.reshape(tile_count, 4, chan_part, side_len).astype(jnp.float32)
        return jnp.sum(got, axis=0)

    def to_pixels(block):
        return lax.all_to_all(block, "ch", 1, 0, tiled=True)

    def to_channels(block):
        return lax.all_to_all(block, "ch", 0, 1, tiled=True)

    def block_forward(block_in, s):
        grid = block_in.reshape(chan_part, side_len, side_len)
        halo = route(border_lines(grid), fwd_pick).astype(jnp.bfloat16)
        halo = jnp.where(own_flip[:, None, None], halo[..., ::-1], halo)
        mixed = depthwise(pad_tile(grid, halo), dk_all[s]).astype(jnp.bfloat16)
        cols = to_pixels(mixed.reshape(chan_part, tile_area))
        normed, inverse_dev, scaled_in = layer_norm(cols.astype(jnp.float32), gain_all[s])
        pre_act = jnp.einsum("ch,cp->hp", up_all[s], scaled_in, preferred_element_type=jnp.float32)
        keeper = keep_mask(drop_seed, s, unit_ids, pixel_ids, hidden)
        dropped = (gelu_value(pre_act) * keeper * drop_scale).astype(jnp.bfloat16)
        branch = jnp.einsum("hc,hp->cp", down_all[s], dropped, preferred_element_type=jnp.float32)
        branch = to_channels(branch)
        out = (
            block_in.astype(jnp.float32) + scale_all[s][:, None] * branch
        ).astype(jnp.bfloat16)
        return out, (normed, inverse_dev, pre_act, keeper)

    def block_backward(grad_out, stored, s):
        normed, inverse_dev, pre_act, keeper = stored
        scaled_grad = (scale_all[s][:, None] * grad_out).astype(jnp.bfloat16)
        cols = to_pixels(scaled_grad)
        grad_drop = jnp.einsum("hc,cp->hp", down_all[s], cols, preferred_element_type=jnp.float32)
        grad_pre = (grad_drop * keeper * drop_scale * gelu_slope(pre_act)).astype(jnp.bfloat16)
        grad_norm = jnp.einsum("ch,hp->cp", up_all[s], grad_pre, preferred_element_type=jnp.float32)
        grad_mixed = norm_back(grad_norm, normed, inverse_dev, gain_all[s])
        grad_mixed = to_channels(grad_mixed).reshape(chan_part, side_len, side_len)
        grad_padded = depth_back(grad_mixed, dk_all[s])
        edge_grad = halo_parts(grad_padded)
        edge_grad = jnp.where(own_flip[:, None, None], edge_grad[..., ::-1], edge_grad).astype(
            jnp.bfloat16
        )
        routed = route(edge_grad, bwd_pick)
        interior = add_border(grad_padded[:, 1:-1, 1:-1], routed)
        return grad_out + interior.reshape(chan_part, tile_area)

    skip_col = skip_scale[:, None]
    current = fields.reshape(chan_part, tile_area)
    outs = []
    stores = []
    for s in range(sections):
        if s == sections - 1:
            current = (
                current.astype(jnp.float32) + skip_col * outs[0].astype(jnp.float32)
            ).astype(jnp.bfloat16)
        current, stored = block_forward(current, s)
        outs.append(current)
        stores.append(stored)
    grads = [None] * sections
    grad_now = cotangent.reshape(chan_part, tile_area).astype(jnp.float32)
    skip_grad = None
    for s in reversed(range(sections)):
        if s == 0 and sections > 1:
            grad_now = grad_now + skip_grad
        grad_now = block_backward(grad_now, stores[s], s)
        grads[s] = grad_now
        if s == sections - 1:
            skip_grad = skip_col * grad_now
    act_keep = outs[0]
    grad_keep = grads[0]
    for s in range(1, sections):
        act_keep = jnp.where(my_phase == s, outs[s], act_keep)
        grad_keep = jnp.where(my_phase == s, grads[s], grad_keep)
    return (
        act_keep.reshape(1, chan_part, tile_dev, tile_area),
        grad_keep.reshape(1, chan_part, tile_dev, tile_area),
    )


def solution(mesh):
    placed = (
        P("ch", "tile", None),
        P("ch", "tile", None),
        P("sec", "ch", None),
        P("sec", None),
        P("sec", None, None),
        P("sec", None, None),
        P("sec", "ch"),
        P("ch"),
        P(),
        P(),
        P("tile"),
        P(),
    )
    return jax.shard_map(
        shards,
        mesh=mesh,
        in_specs=placed,
        out_specs=(P("sec", "ch", "tile", None), P("sec", "ch", "tile", None)),
        check_vma=False,
    )
```

```python
import jax
import jax.numpy as jnp
from jax import lax
from jax.sharding import PartitionSpec as P

SIDE = 32


drop_scale = 1.0 / 0.9
gelu_coeff = 0.7978845608028654
cubic_coeff = 0.044715


def mix_bits(counter):
    counter = counter * jnp.int32(739982445)
    counter = counter ^ lax.shift_right_logical(counter, jnp.int32(15))
    counter = counter * jnp.int32(695872825)
    counter = counter ^ lax.shift_right_logical(counter, jnp.int32(12))
    return counter


def keep_mask(drop_seed, section, unit_ids, pixels, hidden):
    salted = mix_bits(drop_seed + section * jnp.int32(1000003))
    counter = pixels[None, :] * jnp.int32(hidden) + unit_ids[:, None]
    mixed_bits = mix_bits(counter ^ salted)
    return (mixed_bits & jnp.int32(65535) >= jnp.int32(6554)).astype(jnp.float32)


def layer_norm(columns, norm_gain):
    centre = columns - jnp.mean(columns, axis=0, keepdims=True)
    inverse_dev = lax.rsqrt(jnp.mean(centre * centre, axis=0, keepdims=True) + 1e-06)
    normed = centre * inverse_dev
    return (normed, inverse_dev, (normed * norm_gain[:, None]).astype(jnp.bfloat16))


def norm_back(grad_in, normed, inverse_dev, norm_gain):
    scaled = grad_in * norm_gain[:, None]
    return inverse_dev * (
        scaled
        - jnp.mean(scaled, axis=0, keepdims=True)
        - normed * jnp.mean(scaled * normed, axis=0, keepdims=True)
    )


def gelu_value(pre_act):
    tanh_part = jnp.tanh(gelu_coeff * (pre_act + cubic_coeff * pre_act * pre_act * pre_act))
    return 0.5 * pre_act * (1.0 + tanh_part)


def gelu_slope(pre_act):
    tanh_part = jnp.tanh(gelu_coeff * (pre_act + cubic_coeff * pre_act * pre_act * pre_act))
    return 0.5 * (1.0 + tanh_part) + 0.5 * pre_act * (1.0 - tanh_part * tanh_part) * gelu_coeff * (
        1.0 + 3.0 * cubic_coeff * pre_act * pre_act
    )


def border_lines(grid):
    return jnp.stack([grid[:, 0, :], grid[:, -1, :], grid[:, :, 0], grid[:, :, -1]], axis=0)


def pad_tile(grid, halo):
    zero_corner = jnp.zeros(grid.shape[:1] + (1, 1), grid.dtype)
    middle = jnp.concatenate([halo[2][:, :, None], grid, halo[3][:, :, None]], axis=2)
    top_row = jnp.concatenate([zero_corner, halo[0][:, None, :], zero_corner], axis=2)
    bottom_row = jnp.concatenate([zero_corner, halo[1][:, None, :], zero_corner], axis=2)
    return jnp.concatenate([top_row, middle, bottom_row], axis=1)


def depthwise(padded, depth_kernel):
    side_len = padded.shape[1] - 2
    running = jnp.zeros(padded.shape[:1] + (side_len, side_len), jnp.float32)
    for down_step in range(3):
        for right_step in range(3):
            weight_now = depth_kernel[:, down_step * 3 + right_step][:, None, None]
            running = running + weight_now * padded[
                :, down_step : down_step + side_len, right_step : right_step + side_len
            ].astype(jnp.float32)
    return running


def depth_back(grad_in, depth_kernel):
    side_len = grad_in.shape[1]
    widened = jnp.pad(grad_in, ((0, 0), (2, 2), (2, 2)))
    running = jnp.zeros(grad_in.shape[:1] + (side_len + 2, side_len + 2), jnp.float32)
    for down_step in range(3):
        for right_step in range(3):
            weight_now = depth_kernel[:, down_step * 3 + right_step][:, None, None]
            running = running + weight_now * widened[
                :,
                2 - down_step : 4 - down_step + side_len,
                2 - right_step : 4 - right_step + side_len,
            ]
    return running


def halo_parts(padded):
    return jnp.stack(
        [padded[:, 0, 1:-1], padded[:, -1, 1:-1], padded[:, 1:-1, 0], padded[:, 1:-1, -1]], axis=0
    )


def add_border(interior, border):
    last = interior.shape[1] - 1
    top = jnp.pad(border[0][:, None, :], ((0, 0), (0, last), (0, 0)))
    bottom = jnp.pad(border[1][:, None, :], ((0, 0), (last, 0), (0, 0)))
    left = jnp.pad(border[2][:, :, None], ((0, 0), (0, 0), (0, last)))
    right = jnp.pad(border[3][:, :, None], ((0, 0), (0, 0), (last, 0)))
    return interior + top + bottom + left + right


def shards(
    fields,
    cotangent,
    depth_kernel,
    norm_gain,
    up_weight,
    down_weight,
    layer_scale,
    skip_scale,
    neighbours,
    edge_codes,
    offsets,
    drop_seed,
):
    chan_part, tile_dev, tile_area = fields.shape
    assert tile_dev == 1
    side_len = SIDE
    my_phase = lax.axis_index("sec")
    sections = lax.axis_size("sec")
    ch_index = lax.axis_index("ch")
    ch_count = lax.axis_size("ch")
    tile_count = lax.axis_size("tile")
    my_tile = lax.axis_index("tile")
    hidden = up_weight.shape[2]
    pix_part = tile_area // ch_count

    small = jnp.concatenate(
        [depth_kernel[0].reshape(-1), norm_gain[0], layer_scale[0]]
    )
    large = jnp.concatenate([up_weight[0].reshape(-1), down_weight[0].reshape(-1)])
    small_got = [small]
    for shift in range(1, sections):
        route_now = [(i, (i + shift) % sections) for i in range(sections)]
        small_got.append(lax.ppermute(small, "sec", route_now))
    large_got = [large]
    large_sent = []

    def send_large(after):
        after, tied = lax.optimization_barrier((after, large))
        for shift in range(1, sections):
            route_now = [(i, (i + shift) % sections) for i in range(sections)]
            large_got.append(lax.ppermute(tied, "sec", route_now))
        return after

    def section_weights(s, large_got):
        behind = (my_phase - s) % sections
        small_s = small_got[0]
        large_s = large_got[0]
        for shift in range(1, sections):
            small_s = jnp.where(behind == shift, small_got[shift], small_s)
            large_s = jnp.where(behind == shift, large_got[shift], large_s)
        dk_len = chan_part * 9
        cut = up_weight.shape[1] * hidden
        return (
            small_s[:dk_len].reshape(chan_part, 9),
            small_s[dk_len : dk_len + norm_gain.shape[1]],
            small_s[dk_len + norm_gain.shape[1] :],
            large_s[:cut].reshape(up_weight.shape[1:]),
            large_s[cut:].reshape(down_weight.shape[1:]),
        )

    dk_all, gain_all, scale_all, up_all, down_all = [], [], [], [], []

    def unpack_weights():
        for s in range(sections):
            w = section_weights(s, large_got)
            for store, part in zip((dk_all, gain_all, scale_all, up_all, down_all), w):
                store.append(part)

    side_code = edge_codes % 4
    own_flip = edge_codes[my_tile] >= 4
    fwd_pick = (
        (neighbours[:, :, None] == my_tile)
        & (side_code[:, :, None] == jnp.arange(4, dtype=jnp.int32)[None, None, :])
    ).astype(jnp.bfloat16)
    own_nb = neighbours[my_tile]
    own_code = side_code[my_tile]
    bwd_pick = (
        (own_nb[None, None, :] == jnp.arange(tile_count, dtype=jnp.int32)[:, None, None])
        & (own_code[None, None, :] == jnp.arange(4, dtype=jnp.int32)[None, :, None])
    ).astype(jnp.bfloat16)

    pixel_ids = offsets[0] + ch_index * pix_part + jnp.arange(pix_part, dtype=jnp.int32)
    unit_ids = jnp.arange(hidden, dtype=jnp.int32)

    def route(lines, pick):
        send = jnp.einsum("jek,kcs->jecs", pick, lines, preferred_element_type=jnp.float32)
        send = send.astype(jnp.bfloat16).reshape(tile_count, -1)
        got = lax.all_to_all(send, "tile", 0, 0, tiled=True)
        got = got.reshape(tile_count, 4, chan_part, side_len).astype(jnp.float32)
        return jnp.sum(got, axis=0)

    def to_pixels(block):
        return lax.all_to_all(block, "ch", 1, 0, tiled=True)

    def to_channels(block):
        return lax.all_to_all(block, "ch", 0, 1, tiled=True)

    def block_forward(block_in, s):
        grid = block_in.reshape(chan_part, side_len, side_len)
        halo = route(border_lines(grid), fwd_pick).astype(jnp.bfloat16)
        if s == 0:
            halo = send_large(halo)
            unpack_weights()
        halo = jnp.where(own_flip[:, None, None], halo[..., ::-1], halo)
        mixed = depthwise(pad_tile(grid, halo), dk_all[s]).astype(jnp.bfloat16)
        cols = to_pixels(mixed.reshape(chan_part, tile_area))
        normed, inverse_dev, scaled_in = layer_norm(cols.astype(jnp.float32), gain_all[s])
        pre_act = jnp.einsum("ch,cp->hp", up_all[s], scaled_in, preferred_element_type=jnp.float32)
        keeper = keep_mask(drop_seed, s, unit_ids, pixel_ids, hidden)
        dropped = (gelu_value(pre_act) * keeper * drop_scale).astype(jnp.bfloat16)
        branch = jnp.einsum("hc,hp->cp", down_all[s], dropped, preferred_element_type=jnp.float32)
        branch = to_channels(branch)
        out = (
            block_in.astype(jnp.float32) + scale_all[s][:, None] * branch
        ).astype(jnp.bfloat16)
        return out, (normed, inverse_dev, pre_act, keeper)

    def block_backward(grad_out, stored, s):
        normed, inverse_dev, pre_act, keeper = stored
        scaled_grad = (scale_all[s][:, None] * grad_out).astype(jnp.bfloat16)
        cols = to_pixels(scaled_grad)
        grad_drop = jnp.einsum("hc,cp->hp", down_all[s], cols, preferred_element_type=jnp.float32)
        grad_pre = (grad_drop * keeper * drop_scale * gelu_slope(pre_act)).astype(jnp.bfloat16)
        grad_norm = jnp.einsum("ch,hp->cp", up_all[s], grad_pre, preferred_element_type=jnp.float32)
        grad_mixed = norm_back(grad_norm, normed, inverse_dev, gain_all[s])
        grad_mixed = to_channels(grad_mixed).reshape(chan_part, side_len, side_len)
        grad_padded = depth_back(grad_mixed, dk_all[s])
        edge_grad = halo_parts(grad_padded)
        edge_grad = jnp.where(own_flip[:, None, None], edge_grad[..., ::-1], edge_grad).astype(
            jnp.bfloat16
        )
        routed = route(edge_grad, bwd_pick)
        interior = add_border(grad_padded[:, 1:-1, 1:-1], routed)
        return grad_out + interior.reshape(chan_part, tile_area)

    skip_col = skip_scale[:, None]
    current = fields.reshape(chan_part, tile_area)
    outs = []
    stores = []
    for s in range(sections):
        if s == sections - 1:
            current = (
                current.astype(jnp.float32) + skip_col * outs[0].astype(jnp.float32)
            ).astype(jnp.bfloat16)
        current, stored = block_forward(current, s)
        outs.append(current)
        stores.append(stored)
    grads = [None] * sections
    grad_now = cotangent.reshape(chan_part, tile_area).astype(jnp.float32)
    skip_grad = None
    for s in reversed(range(sections)):
        if s == 0 and sections > 1:
            grad_now = grad_now + skip_grad
        grad_now = block_backward(grad_now, stores[s], s)
        grads[s] = grad_now
        if s == sections - 1:
            skip_grad = skip_col * grad_now
    act_keep = outs[0]
    grad_keep = grads[0]
    for s in range(1, sections):
        act_keep = jnp.where(my_phase == s, outs[s], act_keep)
        grad_keep = jnp.where(my_phase == s, grads[s], grad_keep)
    return (
        act_keep.reshape(1, chan_part, tile_dev, tile_area),
        grad_keep.reshape(1, chan_part, tile_dev, tile_area),
    )


def solution(mesh):
    placed = (
        P("ch", "tile", None),
        P("ch", "tile", None),
        P("sec", "ch", None),
        P("sec", None),
        P("sec", None, None),
        P("sec", None, None),
        P("sec", "ch"),
        P("ch"),
        P(),
        P(),
        P("tile"),
        P(),
    )
    return jax.shard_map(
        shards,
        mesh=mesh,
        in_specs=placed,
        out_specs=(P("sec", "ch", "tile", None), P("sec", "ch", "tile", None)),
        check_vma=False,
    )
```

```python
import jax
import jax.numpy as jnp
from jax import lax
from jax.sharding import PartitionSpec as P

SIDE = 32


drop_scale = 1.0 / 0.9
gelu_coeff = 0.7978845608028654
cubic_coeff = 0.044715


def mix_bits(counter):
    counter = counter * jnp.int32(739982445)
    counter = counter ^ lax.shift_right_logical(counter, jnp.int32(15))
    counter = counter * jnp.int32(695872825)
    counter = counter ^ lax.shift_right_logical(counter, jnp.int32(12))
    return counter


def keep_mask(drop_seed, section, unit_ids, pixels, hidden):
    salted = mix_bits(drop_seed + section * jnp.int32(1000003))
    counter = pixels[None, :] * jnp.int32(hidden) + unit_ids[:, None]
    mixed_bits = mix_bits(counter ^ salted)
    return (mixed_bits & jnp.int32(65535) >= jnp.int32(6554)).astype(jnp.float32)


def layer_norm(columns, norm_gain):
    centre = columns - jnp.mean(columns, axis=0, keepdims=True)
    inverse_dev = lax.rsqrt(jnp.mean(centre * centre, axis=0, keepdims=True) + 1e-06)
    normed = centre * inverse_dev
    return (normed, inverse_dev, (normed * norm_gain[:, None]).astype(jnp.bfloat16))


def norm_back(grad_in, normed, inverse_dev, norm_gain):
    scaled = grad_in * norm_gain[:, None]
    return inverse_dev * (
        scaled
        - jnp.mean(scaled, axis=0, keepdims=True)
        - normed * jnp.mean(scaled * normed, axis=0, keepdims=True)
    )


def gelu_value(pre_act):
    tanh_part = jnp.tanh(gelu_coeff * (pre_act + cubic_coeff * pre_act * pre_act * pre_act))
    return 0.5 * pre_act * (1.0 + tanh_part)


def gelu_slope(pre_act):
    tanh_part = jnp.tanh(gelu_coeff * (pre_act + cubic_coeff * pre_act * pre_act * pre_act))
    return 0.5 * (1.0 + tanh_part) + 0.5 * pre_act * (1.0 - tanh_part * tanh_part) * gelu_coeff * (
        1.0 + 3.0 * cubic_coeff * pre_act * pre_act
    )


def border_lines(grid):
    return jnp.stack([grid[:, 0, :], grid[:, -1, :], grid[:, :, 0], grid[:, :, -1]], axis=0)


def pad_tile(grid, halo):
    zero_corner = jnp.zeros(grid.shape[:1] + (1, 1), grid.dtype)
    middle = jnp.concatenate([halo[2][:, :, None], grid, halo[3][:, :, None]], axis=2)
    top_row = jnp.concatenate([zero_corner, halo[0][:, None, :], zero_corner], axis=2)
    bottom_row = jnp.concatenate([zero_corner, halo[1][:, None, :], zero_corner], axis=2)
    return jnp.concatenate([top_row, middle, bottom_row], axis=1)


def depthwise(padded, depth_kernel):
    side_len = padded.shape[1] - 2
    running = jnp.zeros(padded.shape[:1] + (side_len, side_len), jnp.float32)
    for down_step in range(3):
        for right_step in range(3):
            weight_now = depth_kernel[:, down_step * 3 + right_step][:, None, None]
            running = running + weight_now * padded[
                :, down_step : down_step + side_len, right_step : right_step + side_len
            ].astype(jnp.float32)
    return running


def depth_back(grad_in, depth_kernel):
    side_len = grad_in.shape[1]
    widened = jnp.pad(grad_in, ((0, 0), (2, 2), (2, 2)))
    running = jnp.zeros(grad_in.shape[:1] + (side_len + 2, side_len + 2), jnp.float32)
    for down_step in range(3):
        for right_step in range(3):
            weight_now = depth_kernel[:, down_step * 3 + right_step][:, None, None]
            running = running + weight_now * widened[
                :,
                2 - down_step : 4 - down_step + side_len,
                2 - right_step : 4 - right_step + side_len,
            ]
    return running


def halo_parts(padded):
    return jnp.stack(
        [padded[:, 0, 1:-1], padded[:, -1, 1:-1], padded[:, 1:-1, 0], padded[:, 1:-1, -1]], axis=0
    )


def add_border(interior, border):
    last = interior.shape[1] - 1
    top = jnp.pad(border[0][:, None, :], ((0, 0), (0, last), (0, 0)))
    bottom = jnp.pad(border[1][:, None, :], ((0, 0), (last, 0), (0, 0)))
    left = jnp.pad(border[2][:, :, None], ((0, 0), (0, 0), (0, last)))
    right = jnp.pad(border[3][:, :, None], ((0, 0), (0, 0), (last, 0)))
    return interior + top + bottom + left + right


def shards(
    fields,
    cotangent,
    depth_kernel,
    norm_gain,
    up_weight,
    down_weight,
    layer_scale,
    skip_scale,
    neighbours,
    edge_codes,
    offsets,
    drop_seed,
):
    chan_part, tile_dev, tile_area = fields.shape
    assert tile_dev == 1
    side_len = SIDE
    my_phase = lax.axis_index("sec")
    sections = lax.axis_size("sec")
    ch_index = lax.axis_index("ch")
    ch_count = lax.axis_size("ch")
    tile_count = lax.axis_size("tile")
    my_tile = lax.axis_index("tile")
    hidden = up_weight.shape[2]
    pix_part = tile_area // ch_count

    small = jnp.concatenate(
        [depth_kernel[0].reshape(-1), norm_gain[0], layer_scale[0]]
    )
    large = jnp.concatenate([up_weight[0].reshape(-1), down_weight[0].reshape(-1)])
    small_got = [small]
    for shift in range(1, sections):
        route_now = [(i, (i + shift) % sections) for i in range(sections)]
        small_got.append(lax.ppermute(small, "sec", route_now))
    large_got = [large]
    large_sent = []

    def send_large(after):
        after, tied = lax.optimization_barrier((after, large))
        for shift in range(1, sections):
            route_now = [(i, (i + shift) % sections) for i in range(sections)]
            large_got.append(lax.ppermute(tied, "sec", route_now))
        return after

    def section_weights(s, large_got):
        behind = (my_phase - s) % sections
        small_s = small_got[0]
        large_s = large_got[0]
        for shift in range(1, sections):
            small_s = jnp.where(behind == shift, small_got[shift], small_s)
            large_s = jnp.where(behind == shift, large_got[shift], large_s)
        dk_len = chan_part * 9
        cut = up_weight.shape[1] * hidden
        return (
            small_s[:dk_len].reshape(chan_part, 9),
            small_s[dk_len : dk_len + norm_gain.shape[1]],
            small_s[dk_len + norm_gain.shape[1] :],
            large_s[:cut].reshape(up_weight.shape[1:]),
            large_s[cut:].reshape(down_weight.shape[1:]),
        )

    dk_all, gain_all, scale_all, up_all, down_all = [], [], [], [], []

    def unpack_weights():
        for s in range(sections):
            w = section_weights(s, large_got)
            for store, part in zip((dk_all, gain_all, scale_all, up_all, down_all), w):
                store.append(part)

    side_code = edge_codes % 4
    own_flip = edge_codes[my_tile] >= 4
    line_ids = jnp.arange(4, dtype=jnp.int32)
    same_tile = neighbours[:, :, None] == neighbours[:, None, :]
    earlier = line_ids[None, :] < line_ids[:, None]
    rank = jnp.sum((same_tile & earlier[None]).astype(jnp.int32), axis=2)
    narrow = jnp.max(rank) < 2

    def send_pick(width):
        hit = (
            (neighbours == my_tile)[:, :, None, None]
            & (rank[:, :, None, None] == jnp.arange(width, dtype=jnp.int32)[None, None, :, None])
            & (side_code[:, :, None, None] == line_ids[None, None, None, :])
        )
        return jnp.sum(hit.astype(jnp.float32), axis=1).astype(jnp.bfloat16)

    def take_pick(width):
        hit = (
            neighbours[my_tile][:, None, None]
            == jnp.arange(tile_count, dtype=jnp.int32)[None, :, None]
        ) & (rank[my_tile][:, None, None] == jnp.arange(width, dtype=jnp.int32)[None, None, :])
        return hit.astype(jnp.bfloat16)

    pixel_ids = offsets[0] + ch_index * pix_part + jnp.arange(pix_part, dtype=jnp.int32)
    unit_ids = jnp.arange(hidden, dtype=jnp.int32)

    def route_with(width):
        pick = send_pick(width)
        take = take_pick(width)

        def run(lines):
            send = jnp.einsum("jrk,kcs->jrcs", pick, lines, preferred_element_type=jnp.float32)
            send = send.astype(jnp.bfloat16).reshape(tile_count, -1)
            got = lax.all_to_all(send, "tile", 0, 0, tiled=True)
            got = got.reshape(tile_count, width, chan_part, side_len)
            return jnp.einsum("esr,srcx->ecx", take, got, preferred_element_type=jnp.float32)

        return run

    route_narrow = route_with(2)
    route_wide = route_with(4)

    def route(lines):
        return lax.cond(narrow, route_narrow, route_wide, lines)

    def to_pixels(block):
        return lax.all_to_all(block, "ch", 1, 0, tiled=True)

    def to_channels(block):
        return lax.all_to_all(block, "ch", 0, 1, tiled=True)

    def block_forward(block_in, s):
        grid = block_in.reshape(chan_part, side_len, side_len)
        halo = route(border_lines(grid)).astype(jnp.bfloat16)
        if s == 0:
            halo = send_large(halo)
            unpack_weights()
        halo = jnp.where(own_flip[:, None, None], halo[..., ::-1], halo)
        mixed = depthwise(pad_tile(grid, halo), dk_all[s]).astype(jnp.bfloat16)
        cols = to_pixels(mixed.reshape(chan_part, tile_area))
        normed, inverse_dev, scaled_in = layer_norm(cols.astype(jnp.float32), gain_all[s])
        pre_act = jnp.einsum("ch,cp->hp", up_all[s], scaled_in, preferred_element_type=jnp.float32)
        keeper = keep_mask(drop_seed, s, unit_ids, pixel_ids, hidden)
        dropped = (gelu_value(pre_act) * keeper * drop_scale).astype(jnp.bfloat16)
        branch = jnp.einsum("hc,hp->cp", down_all[s], dropped, preferred_element_type=jnp.float32)
        branch = to_channels(branch)
        out = (
            block_in.astype(jnp.float32) + scale_all[s][:, None] * branch
        ).astype(jnp.bfloat16)
        return out, (normed, inverse_dev, pre_act, keeper)

    def block_backward(grad_out, stored, s):
        normed, inverse_dev, pre_act, keeper = stored
        scaled_grad = (scale_all[s][:, None] * grad_out).astype(jnp.bfloat16)
        cols = to_pixels(scaled_grad)
        grad_drop = jnp.einsum("hc,cp->hp", down_all[s], cols, preferred_element_type=jnp.float32)
        grad_pre = (grad_drop * keeper * drop_scale * gelu_slope(pre_act)).astype(jnp.bfloat16)
        grad_norm = jnp.einsum("ch,hp->cp", up_all[s], grad_pre, preferred_element_type=jnp.float32)
        grad_mixed = norm_back(grad_norm, normed, inverse_dev, gain_all[s])
        grad_mixed = to_channels(grad_mixed).reshape(chan_part, side_len, side_len)
        grad_padded = depth_back(grad_mixed, dk_all[s])
        edge_grad = halo_parts(grad_padded)
        edge_grad = jnp.where(own_flip[:, None, None], edge_grad[..., ::-1], edge_grad).astype(
            jnp.bfloat16
        )
        routed = route(edge_grad)
        interior = add_border(grad_padded[:, 1:-1, 1:-1], routed)
        return grad_out + interior.reshape(chan_part, tile_area)

    skip_col = skip_scale[:, None]
    current = fields.reshape(chan_part, tile_area)
    outs = []
    stores = []
    for s in range(sections):
        if s == sections - 1:
            current = (
                current.astype(jnp.float32) + skip_col * outs[0].astype(jnp.float32)
            ).astype(jnp.bfloat16)
        current, stored = block_forward(current, s)
        outs.append(current)
        stores.append(stored)
    grads = [None] * sections
    grad_now = cotangent.reshape(chan_part, tile_area).astype(jnp.float32)
    skip_grad = None
    for s in reversed(range(sections)):
        if s == 0 and sections > 1:
            grad_now = grad_now + skip_grad
        grad_now = block_backward(grad_now, stores[s], s)
        grads[s] = grad_now
        if s == sections - 1:
            skip_grad = skip_col * grad_now
    act_keep = outs[0]
    grad_keep = grads[0]
    for s in range(1, sections):
        act_keep = jnp.where(my_phase == s, outs[s], act_keep)
        grad_keep = jnp.where(my_phase == s, grads[s], grad_keep)
    return (
        act_keep.reshape(1, chan_part, tile_dev, tile_area),
        grad_keep.reshape(1, chan_part, tile_dev, tile_area),
    )


def solution(mesh):
    placed = (
        P("ch", "tile", None),
        P("ch", "tile", None),
        P("sec", "ch", None),
        P("sec", None),
        P("sec", None, None),
        P("sec", None, None),
        P("sec", "ch"),
        P("ch"),
        P(),
        P(),
        P("tile"),
        P(),
    )
    return jax.shard_map(
        shards,
        mesh=mesh,
        in_specs=placed,
        out_specs=(P("sec", "ch", "tile", None), P("sec", "ch", "tile", None)),
        check_vma=False,
    )
```

```python
import jax
import jax.numpy as jnp
from jax import lax
from jax.sharding import PartitionSpec as P

SIDE = 32


drop_scale = 1.0 / 0.9
gelu_coeff = 0.7978845608028654
cubic_coeff = 0.044715


def mix_bits(counter):
    counter = counter * jnp.int32(739982445)
    counter = counter ^ lax.shift_right_logical(counter, jnp.int32(15))
    counter = counter * jnp.int32(695872825)
    counter = counter ^ lax.shift_right_logical(counter, jnp.int32(12))
    return counter


def keep_mask(drop_seed, section, unit_ids, pixels, hidden):
    salted = mix_bits(drop_seed + section * jnp.int32(1000003))
    counter = pixels[None, :] * jnp.int32(hidden) + unit_ids[:, None]
    mixed_bits = mix_bits(counter ^ salted)
    return (mixed_bits & jnp.int32(65535) >= jnp.int32(6554)).astype(jnp.float32)


def layer_norm(columns, norm_gain):
    centre = columns - jnp.mean(columns, axis=0, keepdims=True)
    inverse_dev = lax.rsqrt(jnp.mean(centre * centre, axis=0, keepdims=True) + 1e-06)
    normed = centre * inverse_dev
    return (normed, inverse_dev, (normed * norm_gain[:, None]).astype(jnp.bfloat16))


def norm_back(grad_in, normed, inverse_dev, norm_gain):
    scaled = grad_in * norm_gain[:, None]
    return inverse_dev * (
        scaled
        - jnp.mean(scaled, axis=0, keepdims=True)
        - normed * jnp.mean(scaled * normed, axis=0, keepdims=True)
    )


def gelu_value(pre_act):
    tanh_part = jnp.tanh(gelu_coeff * (pre_act + cubic_coeff * pre_act * pre_act * pre_act))
    return 0.5 * pre_act * (1.0 + tanh_part)


def gelu_slope(pre_act):
    tanh_part = jnp.tanh(gelu_coeff * (pre_act + cubic_coeff * pre_act * pre_act * pre_act))
    return 0.5 * (1.0 + tanh_part) + 0.5 * pre_act * (1.0 - tanh_part * tanh_part) * gelu_coeff * (
        1.0 + 3.0 * cubic_coeff * pre_act * pre_act
    )


def border_lines(grid):
    return jnp.stack([grid[:, 0, :], grid[:, -1, :], grid[:, :, 0], grid[:, :, -1]], axis=0)


def pad_tile(grid, halo):
    zero_corner = jnp.zeros(grid.shape[:1] + (1, 1), grid.dtype)
    middle = jnp.concatenate([halo[2][:, :, None], grid, halo[3][:, :, None]], axis=2)
    top_row = jnp.concatenate([zero_corner, halo[0][:, None, :], zero_corner], axis=2)
    bottom_row = jnp.concatenate([zero_corner, halo[1][:, None, :], zero_corner], axis=2)
    return jnp.concatenate([top_row, middle, bottom_row], axis=1)


def depthwise(padded, depth_kernel):
    side_len = padded.shape[1] - 2
    running = jnp.zeros(padded.shape[:1] + (side_len, side_len), jnp.float32)
    for down_step in range(3):
        for right_step in range(3):
            weight_now = depth_kernel[:, down_step * 3 + right_step][:, None, None]
            running = running + weight_now * padded[
                :, down_step : down_step + side_len, right_step : right_step + side_len
            ].astype(jnp.float32)
    return running


def depth_back(grad_in, depth_kernel):
    side_len = grad_in.shape[1]
    widened = jnp.pad(grad_in, ((0, 0), (2, 2), (2, 2)))
    running = jnp.zeros(grad_in.shape[:1] + (side_len + 2, side_len + 2), jnp.float32)
    for down_step in range(3):
        for right_step in range(3):
            weight_now = depth_kernel[:, down_step * 3 + right_step][:, None, None]
            running = running + weight_now * widened[
                :,
                2 - down_step : 4 - down_step + side_len,
                2 - right_step : 4 - right_step + side_len,
            ]
    return running


def halo_parts(padded):
    return jnp.stack(
        [padded[:, 0, 1:-1], padded[:, -1, 1:-1], padded[:, 1:-1, 0], padded[:, 1:-1, -1]], axis=0
    )


def add_border(interior, border):
    last = interior.shape[1] - 1
    top = jnp.pad(border[0][:, None, :], ((0, 0), (0, last), (0, 0)))
    bottom = jnp.pad(border[1][:, None, :], ((0, 0), (last, 0), (0, 0)))
    left = jnp.pad(border[2][:, :, None], ((0, 0), (0, 0), (0, last)))
    right = jnp.pad(border[3][:, :, None], ((0, 0), (0, 0), (last, 0)))
    return interior + top + bottom + left + right


def shards(
    fields,
    cotangent,
    depth_kernel,
    norm_gain,
    up_weight,
    down_weight,
    layer_scale,
    skip_scale,
    neighbours,
    edge_codes,
    offsets,
    drop_seed,
):
    chan_part, tile_dev, tile_area = fields.shape
    assert tile_dev == 1
    side_len = SIDE
    my_phase = lax.axis_index("sec")
    sections = lax.axis_size("sec")
    ch_index = lax.axis_index("ch")
    ch_count = lax.axis_size("ch")
    tile_count = lax.axis_size("tile")
    my_tile = lax.axis_index("tile")
    hidden = up_weight.shape[2]
    pix_part = tile_area // ch_count

    small = jnp.concatenate([depth_kernel[0].reshape(-1), norm_gain[0], layer_scale[0]])
    small_len = small.shape[0]
    high = small.astype(jnp.bfloat16)
    rest = small - high.astype(jnp.float32)
    middle = rest.astype(jnp.bfloat16)
    low = (rest - middle.astype(jnp.float32)).astype(jnp.bfloat16)
    packed = jnp.concatenate(
        [high, middle, low, up_weight[0].reshape(-1), down_weight[0].reshape(-1)]
    )
    packed_got = [packed]
    for shift in range(1, sections):
        route_now = [(i, (i + shift) % sections) for i in range(sections)]
        packed_got.append(lax.ppermute(packed, "sec", route_now))

    def section_weights(s):
        behind = (my_phase - s) % sections
        got = packed_got[0]
        for shift in range(1, sections):
            got = jnp.where(behind == shift, packed_got[shift], got)
        small_s = (
            got[:small_len].astype(jnp.float32) + got[small_len : 2 * small_len].astype(jnp.float32)
        ) + got[2 * small_len : 3 * small_len].astype(jnp.float32)
        large_s = got[3 * small_len :]
        dk_len = chan_part * 9
        cut = up_weight.shape[1] * hidden
        return (
            small_s[:dk_len].reshape(chan_part, 9),
            small_s[dk_len : dk_len + norm_gain.shape[1]],
            small_s[dk_len + norm_gain.shape[1] :],
            large_s[:cut].reshape(up_weight.shape[1:]),
            large_s[cut:].reshape(down_weight.shape[1:]),
        )

    dk_all, gain_all, scale_all, up_all, down_all = [], [], [], [], []
    for s in range(sections):
        for store, part in zip((dk_all, gain_all, scale_all, up_all, down_all), section_weights(s)):
            store.append(part)

    side_code = edge_codes % 4
    own_flip = edge_codes[my_tile] >= 4
    line_ids = jnp.arange(4, dtype=jnp.int32)
    same_tile = neighbours[:, :, None] == neighbours[:, None, :]
    earlier = line_ids[None, :] < line_ids[:, None]
    rank = jnp.sum((same_tile & earlier[None]).astype(jnp.int32), axis=2)
    narrow = jnp.max(rank) < 2

    def send_pick(width):
        hit = (
            (neighbours == my_tile)[:, :, None, None]
            & (rank[:, :, None, None] == jnp.arange(width, dtype=jnp.int32)[None, None, :, None])
            & (side_code[:, :, None, None] == line_ids[None, None, None, :])
        )
        return jnp.sum(hit.astype(jnp.float32), axis=1).astype(jnp.bfloat16)

    def take_pick(width):
        hit = (
            neighbours[my_tile][:, None, None]
            == jnp.arange(tile_count, dtype=jnp.int32)[None, :, None]
        ) & (rank[my_tile][:, None, None] == jnp.arange(width, dtype=jnp.int32)[None, None, :])
        return hit.astype(jnp.bfloat16)

    pixel_ids = offsets[0] + ch_index * pix_part + jnp.arange(pix_part, dtype=jnp.int32)
    unit_ids = jnp.arange(hidden, dtype=jnp.int32)

    def route_with(width):
        pick = send_pick(width)
        take = take_pick(width)

        def run(lines):
            send = jnp.einsum("jrk,kcs->jrcs", pick, lines, preferred_element_type=jnp.float32)
            send = send.astype(jnp.bfloat16).reshape(tile_count, -1)
            got = lax.all_to_all(send, "tile", 0, 0, tiled=True)
            got = got.reshape(tile_count, width, chan_part, side_len)
            return jnp.einsum("esr,srcx->ecx", take, got, preferred_element_type=jnp.float32)

        return run

    route_narrow = route_with(2)
    route_wide = route_with(4)

    def route(lines):
        return lax.cond(narrow, route_narrow, route_wide, lines)

    def to_pixels(block):
        return lax.all_to_all(block, "ch", 1, 0, tiled=True)

    def to_channels(block):
        return lax.all_to_all(block, "ch", 0, 1, tiled=True)

    def block_forward(block_in, s):
        grid = block_in.reshape(chan_part, side_len, side_len)
        halo = route(border_lines(grid)).astype(jnp.bfloat16)
        halo = jnp.where(own_flip[:, None, None], halo[..., ::-1], halo)
        mixed = depthwise(pad_tile(grid, halo), dk_all[s]).astype(jnp.bfloat16)
        cols = to_pixels(mixed.reshape(chan_part, tile_area))
        normed, inverse_dev, scaled_in = layer_norm(cols.astype(jnp.float32), gain_all[s])
        pre_act = jnp.einsum("ch,cp->hp", up_all[s], scaled_in, preferred_element_type=jnp.float32)
        keeper = keep_mask(drop_seed, s, unit_ids, pixel_ids, hidden)
        dropped = (gelu_value(pre_act) * keeper * drop_scale).astype(jnp.bfloat16)
        branch = jnp.einsum("hc,hp->cp", down_all[s], dropped, preferred_element_type=jnp.float32)
        branch = to_channels(branch)
        out = (
            block_in.astype(jnp.float32) + scale_all[s][:, None] * branch
        ).astype(jnp.bfloat16)
        return out, (normed, inverse_dev, pre_act, keeper)

    def block_backward(grad_out, stored, s):
        normed, inverse_dev, pre_act, keeper = stored
        scaled_grad = (scale_all[s][:, None] * grad_out).astype(jnp.bfloat16)
        cols = to_pixels(scaled_grad)
        grad_drop = jnp.einsum("hc,cp->hp", down_all[s], cols, preferred_element_type=jnp.float32)
        grad_pre = (grad_drop * keeper * drop_scale * gelu_slope(pre_act)).astype(jnp.bfloat16)
        grad_norm = jnp.einsum("ch,hp->cp", up_all[s], grad_pre, preferred_element_type=jnp.float32)
        grad_mixed = norm_back(grad_norm, normed, inverse_dev, gain_all[s])
        grad_mixed = to_channels(grad_mixed).reshape(chan_part, side_len, side_len)
        grad_padded = depth_back(grad_mixed, dk_all[s])
        edge_grad = halo_parts(grad_padded)
        edge_grad = jnp.where(own_flip[:, None, None], edge_grad[..., ::-1], edge_grad).astype(
            jnp.bfloat16
        )
        routed = route(edge_grad)
        interior = add_border(grad_padded[:, 1:-1, 1:-1], routed)
        return grad_out + interior.reshape(chan_part, tile_area)

    skip_col = skip_scale[:, None]
    current = fields.reshape(chan_part, tile_area)
    outs = []
    stores = []
    for s in range(sections):
        if s == sections - 1:
            current = (
                current.astype(jnp.float32) + skip_col * outs[0].astype(jnp.float32)
            ).astype(jnp.bfloat16)
        current, stored = block_forward(current, s)
        outs.append(current)
        stores.append(stored)
    grads = [None] * sections
    grad_now = cotangent.reshape(chan_part, tile_area).astype(jnp.float32)
    skip_grad = None
    for s in reversed(range(sections)):
        if s == 0 and sections > 1:
            grad_now = grad_now + skip_grad
        grad_now = block_backward(grad_now, stores[s], s)
        grads[s] = grad_now
        if s == sections - 1:
            skip_grad = skip_col * grad_now
    act_keep = outs[0]
    grad_keep = grads[0]
    for s in range(1, sections):
        act_keep = jnp.where(my_phase == s, outs[s], act_keep)
        grad_keep = jnp.where(my_phase == s, grads[s], grad_keep)
    return (
        act_keep.reshape(1, chan_part, tile_dev, tile_area),
        grad_keep.reshape(1, chan_part, tile_dev, tile_area),
    )


def solution(mesh):
    placed = (
        P("ch", "tile", None),
        P("ch", "tile", None),
        P("sec", "ch", None),
        P("sec", None),
        P("sec", None, None),
        P("sec", None, None),
        P("sec", "ch"),
        P("ch"),
        P(),
        P(),
        P("tile"),
        P(),
    )
    return jax.shard_map(
        shards,
        mesh=mesh,
        in_specs=placed,
        out_specs=(P("sec", "ch", "tile", None), P("sec", "ch", "tile", None)),
        check_vma=False,
    )
```

```python
import jax
import jax.numpy as jnp
from jax import lax
from jax.sharding import PartitionSpec as P

SIDE = 32


drop_scale = 1.0 / 0.9
gelu_coeff = 0.7978845608028654
cubic_coeff = 0.044715


def mix_bits(counter):
    counter = counter * jnp.int32(739982445)
    counter = counter ^ lax.shift_right_logical(counter, jnp.int32(15))
    counter = counter * jnp.int32(695872825)
    counter = counter ^ lax.shift_right_logical(counter, jnp.int32(12))
    return counter


def keep_mask(drop_seed, section, unit_ids, pixels, hidden):
    salted = mix_bits(drop_seed + section * jnp.int32(1000003))
    counter = pixels[None, :] * jnp.int32(hidden) + unit_ids[:, None]
    mixed_bits = mix_bits(counter ^ salted)
    return (mixed_bits & jnp.int32(65535) >= jnp.int32(6554)).astype(jnp.float32)


def layer_norm(columns, norm_gain):
    centre = columns - jnp.mean(columns, axis=0, keepdims=True)
    inverse_dev = lax.rsqrt(jnp.mean(centre * centre, axis=0, keepdims=True) + 1e-06)
    normed = centre * inverse_dev
    return (normed, inverse_dev, (normed * norm_gain[:, None]).astype(jnp.bfloat16))


def norm_back(grad_in, normed, inverse_dev, norm_gain):
    scaled = grad_in * norm_gain[:, None]
    return inverse_dev * (
        scaled
        - jnp.mean(scaled, axis=0, keepdims=True)
        - normed * jnp.mean(scaled * normed, axis=0, keepdims=True)
    )


def gelu_value(pre_act):
    tanh_part = jnp.tanh(gelu_coeff * (pre_act + cubic_coeff * pre_act * pre_act * pre_act))
    return 0.5 * pre_act * (1.0 + tanh_part)


def gelu_slope(pre_act):
    tanh_part = jnp.tanh(gelu_coeff * (pre_act + cubic_coeff * pre_act * pre_act * pre_act))
    return 0.5 * (1.0 + tanh_part) + 0.5 * pre_act * (1.0 - tanh_part * tanh_part) * gelu_coeff * (
        1.0 + 3.0 * cubic_coeff * pre_act * pre_act
    )


def border_lines(grid):
    return jnp.stack([grid[:, 0, :], grid[:, -1, :], grid[:, :, 0], grid[:, :, -1]], axis=0)


def pad_tile(grid, halo):
    zero_corner = jnp.zeros(grid.shape[:1] + (1, 1), grid.dtype)
    middle = jnp.concatenate([halo[2][:, :, None], grid, halo[3][:, :, None]], axis=2)
    top_row = jnp.concatenate([zero_corner, halo[0][:, None, :], zero_corner], axis=2)
    bottom_row = jnp.concatenate([zero_corner, halo[1][:, None, :], zero_corner], axis=2)
    return jnp.concatenate([top_row, middle, bottom_row], axis=1)


def depthwise(padded, depth_kernel):
    side_len = padded.shape[1] - 2
    running = jnp.zeros(padded.shape[:1] + (side_len, side_len), jnp.float32)
    for down_step in range(3):
        for right_step in range(3):
            weight_now = depth_kernel[:, down_step * 3 + right_step][:, None, None]
            running = running + weight_now * padded[
                :, down_step : down_step + side_len, right_step : right_step + side_len
            ].astype(jnp.float32)
    return running


def depth_back(grad_in, depth_kernel):
    side_len = grad_in.shape[1]
    widened = jnp.pad(grad_in, ((0, 0), (2, 2), (2, 2)))
    running = jnp.zeros(grad_in.shape[:1] + (side_len + 2, side_len + 2), jnp.float32)
    for down_step in range(3):
        for right_step in range(3):
            weight_now = depth_kernel[:, down_step * 3 + right_step][:, None, None]
            running = running + weight_now * widened[
                :,
                2 - down_step : 4 - down_step + side_len,
                2 - right_step : 4 - right_step + side_len,
            ]
    return running


def halo_parts(padded):
    return jnp.stack(
        [padded[:, 0, 1:-1], padded[:, -1, 1:-1], padded[:, 1:-1, 0], padded[:, 1:-1, -1]], axis=0
    )


def add_border(interior, border):
    last = interior.shape[1] - 1
    top = jnp.pad(border[0][:, None, :], ((0, 0), (0, last), (0, 0)))
    bottom = jnp.pad(border[1][:, None, :], ((0, 0), (last, 0), (0, 0)))
    left = jnp.pad(border[2][:, :, None], ((0, 0), (0, 0), (0, last)))
    right = jnp.pad(border[3][:, :, None], ((0, 0), (0, 0), (last, 0)))
    return interior + top + bottom + left + right


def shards(
    fields,
    cotangent,
    depth_kernel,
    norm_gain,
    up_weight,
    down_weight,
    layer_scale,
    skip_scale,
    neighbours,
    edge_codes,
    offsets,
    drop_seed,
):
    chan_part, tile_dev, tile_area = fields.shape
    assert tile_dev == 1
    side_len = SIDE
    my_phase = lax.axis_index("sec")
    sections = lax.axis_size("sec")
    ch_index = lax.axis_index("ch")
    ch_count = lax.axis_size("ch")
    tile_count = lax.axis_size("tile")
    my_tile = lax.axis_index("tile")
    hidden = up_weight.shape[2]
    pix_part = tile_area // ch_count

    small = jnp.concatenate([depth_kernel[0].reshape(-1), norm_gain[0], layer_scale[0]])
    small_len = small.shape[0]
    high = lax.reduce_precision(small, exponent_bits=8, mantissa_bits=7)
    rest = small - high
    middle = lax.reduce_precision(rest, exponent_bits=8, mantissa_bits=7)
    low = lax.reduce_precision(rest - middle, exponent_bits=8, mantissa_bits=7)
    parts = jnp.concatenate([high, middle, low]).astype(jnp.bfloat16)
    packed = jnp.concatenate([parts, up_weight[0].reshape(-1), down_weight[0].reshape(-1)])
    packed_got = [packed]
    for shift in range(1, sections):
        route_now = [(i, (i + shift) % sections) for i in range(sections)]
        packed_got.append(lax.ppermute(packed, "sec", route_now))

    def section_weights(s):
        behind = (my_phase - s) % sections
        got = packed_got[0]
        for shift in range(1, sections):
            got = jnp.where(behind == shift, packed_got[shift], got)
        small_s = (
            got[:small_len].astype(jnp.float32) + got[small_len : 2 * small_len].astype(jnp.float32)
        ) + got[2 * small_len : 3 * small_len].astype(jnp.float32)
        large_s = got[3 * small_len :]
        dk_len = chan_part * 9
        cut = up_weight.shape[1] * hidden
        return (
            small_s[:dk_len].reshape(chan_part, 9),
            small_s[dk_len : dk_len + norm_gain.shape[1]],
            small_s[dk_len + norm_gain.shape[1] :],
            large_s[:cut].reshape(up_weight.shape[1:]),
            large_s[cut:].reshape(down_weight.shape[1:]),
        )

    dk_all, gain_all, scale_all, up_all, down_all = [], [], [], [], []
    for s in range(sections):
        for store, part in zip((dk_all, gain_all, scale_all, up_all, down_all), section_weights(s)):
            store.append(part)

    side_code = edge_codes % 4
    own_flip = edge_codes[my_tile] >= 4
    line_ids = jnp.arange(4, dtype=jnp.int32)
    same_tile = neighbours[:, :, None] == neighbours[:, None, :]
    earlier = line_ids[None, :] < line_ids[:, None]
    rank = jnp.sum((same_tile & earlier[None]).astype(jnp.int32), axis=2)
    narrow = jnp.max(rank) < 2

    def send_pick(width):
        hit = (
            (neighbours == my_tile)[:, :, None, None]
            & (rank[:, :, None, None] == jnp.arange(width, dtype=jnp.int32)[None, None, :, None])
            & (side_code[:, :, None, None] == line_ids[None, None, None, :])
        )
        return jnp.sum(hit.astype(jnp.float32), axis=1).astype(jnp.bfloat16)

    def take_pick(width):
        hit = (
            neighbours[my_tile][:, None, None]
            == jnp.arange(tile_count, dtype=jnp.int32)[None, :, None]
        ) & (rank[my_tile][:, None, None] == jnp.arange(width, dtype=jnp.int32)[None, None, :])
        return hit.astype(jnp.bfloat16)

    pixel_ids = offsets[0] + ch_index * pix_part + jnp.arange(pix_part, dtype=jnp.int32)
    unit_ids = jnp.arange(hidden, dtype=jnp.int32)

    def route_with(width):
        pick = send_pick(width)
        take = take_pick(width)

        def run(lines):
            send = jnp.einsum("jrk,kcs->jrcs", pick, lines, preferred_element_type=jnp.float32)
            send = send.astype(jnp.bfloat16).reshape(tile_count, -1)
            got = lax.all_to_all(send, "tile", 0, 0, tiled=True)
            got = got.reshape(tile_count, width, chan_part, side_len)
            return jnp.einsum("esr,srcx->ecx", take, got, preferred_element_type=jnp.float32)

        return run

    route_narrow = route_with(2)
    route_wide = route_with(4)

    def route(lines):
        return lax.cond(narrow, route_narrow, route_wide, lines)

    def to_pixels(block):
        return lax.all_to_all(block, "ch", 1, 0, tiled=True)

    def to_channels(block):
        return lax.all_to_all(block, "ch", 0, 1, tiled=True)

    def block_forward(block_in, s):
        grid = block_in.reshape(chan_part, side_len, side_len)
        halo = route(border_lines(grid)).astype(jnp.bfloat16)
        halo = jnp.where(own_flip[:, None, None], halo[..., ::-1], halo)
        mixed = depthwise(pad_tile(grid, halo), dk_all[s]).astype(jnp.bfloat16)
        cols = to_pixels(mixed.reshape(chan_part, tile_area))
        normed, inverse_dev, scaled_in = layer_norm(cols.astype(jnp.float32), gain_all[s])
        pre_act = jnp.einsum("ch,cp->hp", up_all[s], scaled_in, preferred_element_type=jnp.float32)
        keeper = keep_mask(drop_seed, s, unit_ids, pixel_ids, hidden)
        dropped = (gelu_value(pre_act) * keeper * drop_scale).astype(jnp.bfloat16)
        branch = jnp.einsum("hc,hp->cp", down_all[s], dropped, preferred_element_type=jnp.float32)
        branch = to_channels(branch)
        out = (
            block_in.astype(jnp.float32) + scale_all[s][:, None] * branch
        ).astype(jnp.bfloat16)
        return out, (normed, inverse_dev, pre_act, keeper)

    def block_backward(grad_out, stored, s):
        normed, inverse_dev, pre_act, keeper = stored
        scaled_grad = (scale_all[s][:, None] * grad_out).astype(jnp.bfloat16)
        cols = to_pixels(scaled_grad)
        grad_drop = jnp.einsum("hc,cp->hp", down_all[s], cols, preferred_element_type=jnp.float32)
        grad_pre = (grad_drop * keeper * drop_scale * gelu_slope(pre_act)).astype(jnp.bfloat16)
        grad_norm = jnp.einsum("ch,hp->cp", up_all[s], grad_pre, preferred_element_type=jnp.float32)
        grad_mixed = norm_back(grad_norm, normed, inverse_dev, gain_all[s])
        grad_mixed = to_channels(grad_mixed).reshape(chan_part, side_len, side_len)
        grad_padded = depth_back(grad_mixed, dk_all[s])
        edge_grad = halo_parts(grad_padded)
        edge_grad = jnp.where(own_flip[:, None, None], edge_grad[..., ::-1], edge_grad).astype(
            jnp.bfloat16
        )
        routed = route(edge_grad)
        interior = add_border(grad_padded[:, 1:-1, 1:-1], routed)
        return grad_out + interior.reshape(chan_part, tile_area)

    skip_col = skip_scale[:, None]
    current = fields.reshape(chan_part, tile_area)
    outs = []
    stores = []
    for s in range(sections):
        if s == sections - 1:
            current = (
                current.astype(jnp.float32) + skip_col * outs[0].astype(jnp.float32)
            ).astype(jnp.bfloat16)
        current, stored = block_forward(current, s)
        outs.append(current)
        stores.append(stored)
    grads = [None] * sections
    grad_now = cotangent.reshape(chan_part, tile_area).astype(jnp.float32)
    skip_grad = None
    for s in reversed(range(sections)):
        if s == 0 and sections > 1:
            grad_now = grad_now + skip_grad
        grad_now = block_backward(grad_now, stores[s], s)
        grads[s] = grad_now
        if s == sections - 1:
            skip_grad = skip_col * grad_now
    act_keep = outs[0]
    grad_keep = grads[0]
    for s in range(1, sections):
        act_keep = jnp.where(my_phase == s, outs[s], act_keep)
        grad_keep = jnp.where(my_phase == s, grads[s], grad_keep)
    return (
        act_keep.reshape(1, chan_part, tile_dev, tile_area),
        grad_keep.reshape(1, chan_part, tile_dev, tile_area),
    )


def solution(mesh):
    placed = (
        P("ch", "tile", None),
        P("ch", "tile", None),
        P("sec", "ch", None),
        P("sec", None),
        P("sec", None, None),
        P("sec", None, None),
        P("sec", "ch"),
        P("ch"),
        P(),
        P(),
        P("tile"),
        P(),
    )
    return jax.shard_map(
        shards,
        mesh=mesh,
        in_specs=placed,
        out_specs=(P("sec", "ch", "tile", None), P("sec", "ch", "tile", None)),
        check_vma=False,
    )
```

```python
import jax
import jax.numpy as jnp
from jax import lax
from jax.sharding import PartitionSpec as P

SIDE = 32


drop_scale = 1.0 / 0.9
gelu_coeff = 0.7978845608028654
cubic_coeff = 0.044715


def mix_bits(counter):
    counter = counter * jnp.int32(739982445)
    counter = counter ^ lax.shift_right_logical(counter, jnp.int32(15))
    counter = counter * jnp.int32(695872825)
    counter = counter ^ lax.shift_right_logical(counter, jnp.int32(12))
    return counter


def keep_mask(drop_seed, section, unit_ids, pixels, hidden):
    salted = mix_bits(drop_seed + section * jnp.int32(1000003))
    counter = pixels[None, :] * jnp.int32(hidden) + unit_ids[:, None]
    mixed_bits = mix_bits(counter ^ salted)
    return (mixed_bits & jnp.int32(65535) >= jnp.int32(6554)).astype(jnp.float32)


def layer_norm(columns, norm_gain):
    centre = columns - jnp.mean(columns, axis=0, keepdims=True)
    inverse_dev = lax.rsqrt(jnp.mean(centre * centre, axis=0, keepdims=True) + 1e-06)
    normed = centre * inverse_dev
    return (normed, inverse_dev, (normed * norm_gain[:, None]).astype(jnp.bfloat16))


def norm_back(grad_in, normed, inverse_dev, norm_gain):
    scaled = grad_in * norm_gain[:, None]
    return inverse_dev * (
        scaled
        - jnp.mean(scaled, axis=0, keepdims=True)
        - normed * jnp.mean(scaled * normed, axis=0, keepdims=True)
    )


def gelu_value(pre_act):
    tanh_part = jnp.tanh(gelu_coeff * (pre_act + cubic_coeff * pre_act * pre_act * pre_act))
    return 0.5 * pre_act * (1.0 + tanh_part)


def gelu_slope(pre_act):
    tanh_part = jnp.tanh(gelu_coeff * (pre_act + cubic_coeff * pre_act * pre_act * pre_act))
    return 0.5 * (1.0 + tanh_part) + 0.5 * pre_act * (1.0 - tanh_part * tanh_part) * gelu_coeff * (
        1.0 + 3.0 * cubic_coeff * pre_act * pre_act
    )


def border_lines(grid):
    return jnp.stack([grid[:, 0, :], grid[:, -1, :], grid[:, :, 0], grid[:, :, -1]], axis=0)


def pad_tile(grid, halo):
    zero_corner = jnp.zeros(grid.shape[:1] + (1, 1), grid.dtype)
    middle = jnp.concatenate([halo[2][:, :, None], grid, halo[3][:, :, None]], axis=2)
    top_row = jnp.concatenate([zero_corner, halo[0][:, None, :], zero_corner], axis=2)
    bottom_row = jnp.concatenate([zero_corner, halo[1][:, None, :], zero_corner], axis=2)
    return jnp.concatenate([top_row, middle, bottom_row], axis=1)


def depthwise(padded, depth_kernel):
    side_len = padded.shape[1] - 2
    running = jnp.zeros(padded.shape[:1] + (side_len, side_len), jnp.float32)
    for down_step in range(3):
        for right_step in range(3):
            weight_now = depth_kernel[:, down_step * 3 + right_step][:, None, None]
            running = running + weight_now * padded[
                :, down_step : down_step + side_len, right_step : right_step + side_len
            ].astype(jnp.float32)
    return running


def depth_back(grad_in, depth_kernel):
    side_len = grad_in.shape[1]
    widened = jnp.pad(grad_in, ((0, 0), (2, 2), (2, 2)))
    running = jnp.zeros(grad_in.shape[:1] + (side_len + 2, side_len + 2), jnp.float32)
    for down_step in range(3):
        for right_step in range(3):
            weight_now = depth_kernel[:, down_step * 3 + right_step][:, None, None]
            running = running + weight_now * widened[
                :,
                2 - down_step : 4 - down_step + side_len,
                2 - right_step : 4 - right_step + side_len,
            ]
    return running


def halo_parts(padded):
    return jnp.stack(
        [padded[:, 0, 1:-1], padded[:, -1, 1:-1], padded[:, 1:-1, 0], padded[:, 1:-1, -1]], axis=0
    )


def add_border(interior, border):
    last = interior.shape[1] - 1
    top = jnp.pad(border[0][:, None, :], ((0, 0), (0, last), (0, 0)))
    bottom = jnp.pad(border[1][:, None, :], ((0, 0), (last, 0), (0, 0)))
    left = jnp.pad(border[2][:, :, None], ((0, 0), (0, 0), (0, last)))
    right = jnp.pad(border[3][:, :, None], ((0, 0), (0, 0), (last, 0)))
    return interior + top + bottom + left + right


def shards(
    fields,
    cotangent,
    depth_kernel,
    norm_gain,
    up_weight,
    down_weight,
    layer_scale,
    skip_scale,
    neighbours,
    edge_codes,
    offsets,
    drop_seed,
):
    chan_part, tile_dev, tile_area = fields.shape
    assert tile_dev == 1
    side_len = SIDE
    my_phase = lax.axis_index("sec")
    sections = lax.axis_size("sec")
    ch_index = lax.axis_index("ch")
    ch_count = lax.axis_size("ch")
    tile_count = lax.axis_size("tile")
    my_tile = lax.axis_index("tile")
    hidden = up_weight.shape[2]
    pix_part = tile_area // ch_count

    small = jnp.concatenate([depth_kernel[0].reshape(-1), norm_gain[0], layer_scale[0]])
    small_len = small.shape[0]
    high = lax.reduce_precision(small, exponent_bits=8, mantissa_bits=7)
    rest = small - high
    middle = lax.reduce_precision(rest, exponent_bits=8, mantissa_bits=7)
    low = lax.reduce_precision(rest - middle, exponent_bits=8, mantissa_bits=7)
    parts = jnp.concatenate([high, middle, low]).astype(jnp.bfloat16)
    packed = jnp.concatenate([parts, up_weight[0].reshape(-1), down_weight[0].reshape(-1)])
    packed_got = [packed]
    for shift in range(1, sections):
        route_now = [(i, (i + shift) % sections) for i in range(sections)]
        packed_got.append(lax.ppermute(packed, "sec", route_now))

    def section_weights(s):
        behind = (my_phase - s) % sections
        got = packed_got[0]
        for shift in range(1, sections):
            got = jnp.where(behind == shift, packed_got[shift], got)
        small_s = (
            got[:small_len].astype(jnp.float32) + got[small_len : 2 * small_len].astype(jnp.float32)
        ) + got[2 * small_len : 3 * small_len].astype(jnp.float32)
        large_s = got[3 * small_len :]
        dk_len = chan_part * 9
        cut = up_weight.shape[1] * hidden
        return (
            small_s[:dk_len].reshape(chan_part, 9),
            small_s[dk_len : dk_len + norm_gain.shape[1]],
            small_s[dk_len + norm_gain.shape[1] :],
            large_s[:cut].reshape(up_weight.shape[1:]),
            large_s[cut:].reshape(down_weight.shape[1:]),
        )

    dk_all, gain_all, scale_all, up_all, down_all = [], [], [], [], []
    for s in range(sections):
        for store, part in zip((dk_all, gain_all, scale_all, up_all, down_all), section_weights(s)):
            store.append(part)

    side_code = edge_codes % 4
    own_flip = edge_codes[my_tile] >= 4
    line_ids = jnp.arange(4, dtype=jnp.int32)
    same_tile = neighbours[:, :, None] == neighbours[:, None, :]
    earlier = line_ids[None, :] < line_ids[:, None]
    rank = jnp.sum((same_tile & earlier[None]).astype(jnp.int32), axis=2)
    narrow = jnp.max(rank) < 2

    def send_pick(width):
        hit = (
            (neighbours == my_tile)[:, :, None, None]
            & (rank[:, :, None, None] == jnp.arange(width, dtype=jnp.int32)[None, None, :, None])
            & (side_code[:, :, None, None] == line_ids[None, None, None, :])
        )
        return jnp.sum(hit.astype(jnp.float32), axis=1).astype(jnp.bfloat16)

    def take_pick(width):
        hit = (
            neighbours[my_tile][:, None, None]
            == jnp.arange(tile_count, dtype=jnp.int32)[None, :, None]
        ) & (rank[my_tile][:, None, None] == jnp.arange(width, dtype=jnp.int32)[None, None, :])
        return hit.astype(jnp.bfloat16)

    pixel_ids = offsets[0] + ch_index * pix_part + jnp.arange(pix_part, dtype=jnp.int32)
    unit_ids = jnp.arange(hidden, dtype=jnp.int32)

    def route_with(width):
        pick = send_pick(width)
        take = take_pick(width)

        def run(lines):
            send = jnp.einsum("jrk,kcs->jrcs", pick, lines, preferred_element_type=jnp.float32)
            send = send.astype(jnp.bfloat16).reshape(tile_count, -1)
            got = lax.all_to_all(send, "tile", 0, 0, tiled=True)
            got = got.reshape(tile_count, width, chan_part, side_len)
            return jnp.einsum("esr,srcx->ecx", take, got, preferred_element_type=jnp.float32)

        return run

    route_narrow = route_with(2)
    route_wide = route_with(4)

    def route(lines):
        return lax.cond(narrow, route_narrow, route_wide, lines)

    def to_pixels(block):
        return lax.all_to_all(block, "ch", 1, 0, tiled=True)

    def to_channels(block):
        return lax.all_to_all(block, "ch", 0, 1, tiled=True)

    def block_forward(block_in, s):
        grid = block_in.reshape(chan_part, side_len, side_len)
        halo = route(border_lines(grid)).astype(jnp.bfloat16)
        halo = jnp.where(own_flip[:, None, None], halo[..., ::-1], halo)
        mixed = depthwise(pad_tile(grid, halo), dk_all[s]).astype(jnp.bfloat16)
        mixed = mixed.reshape(chan_part, tile_area)
        if s == 0:
            both = jnp.stack([mixed, last_scaled]).reshape(2, chan_part, ch_count, pix_part)
            both = lax.all_to_all(both, "ch", 2, 1, tiled=True)
            cols = both[0].reshape(-1, pix_part)
            early_cols.append(both[1].reshape(-1, pix_part))
        else:
            cols = to_pixels(mixed)
        normed, inverse_dev, scaled_in = layer_norm(cols.astype(jnp.float32), gain_all[s])
        pre_act = jnp.einsum("ch,cp->hp", up_all[s], scaled_in, preferred_element_type=jnp.float32)
        keeper = keep_mask(drop_seed, s, unit_ids, pixel_ids, hidden)
        dropped = (gelu_value(pre_act) * keeper * drop_scale).astype(jnp.bfloat16)
        branch = jnp.einsum("hc,hp->cp", down_all[s], dropped, preferred_element_type=jnp.float32)
        branch = to_channels(branch)
        out = (
            block_in.astype(jnp.float32) + scale_all[s][:, None] * branch
        ).astype(jnp.bfloat16)
        return out, (normed, inverse_dev, pre_act, keeper)

    def block_backward(grad_out, stored, s):
        normed, inverse_dev, pre_act, keeper = stored
        if s == sections - 1:
            cols = early_cols[0]
        else:
            scaled_grad = (scale_all[s][:, None] * grad_out).astype(jnp.bfloat16)
            cols = to_pixels(scaled_grad)
        grad_drop = jnp.einsum("hc,cp->hp", down_all[s], cols, preferred_element_type=jnp.float32)
        grad_pre = (grad_drop * keeper * drop_scale * gelu_slope(pre_act)).astype(jnp.bfloat16)
        grad_norm = jnp.einsum("ch,hp->cp", up_all[s], grad_pre, preferred_element_type=jnp.float32)
        grad_mixed = norm_back(grad_norm, normed, inverse_dev, gain_all[s])
        grad_mixed = to_channels(grad_mixed).reshape(chan_part, side_len, side_len)
        grad_padded = depth_back(grad_mixed, dk_all[s])
        edge_grad = halo_parts(grad_padded)
        edge_grad = jnp.where(own_flip[:, None, None], edge_grad[..., ::-1], edge_grad).astype(
            jnp.bfloat16
        )
        routed = route(edge_grad)
        interior = add_border(grad_padded[:, 1:-1, 1:-1], routed)
        return grad_out + interior.reshape(chan_part, tile_area)

    skip_col = skip_scale[:, None]
    cot_full = cotangent.reshape(chan_part, tile_area).astype(jnp.float32)
    last_scaled = (scale_all[sections - 1][:, None] * cot_full).astype(jnp.bfloat16)
    early_cols = []
    current = fields.reshape(chan_part, tile_area)
    outs = []
    stores = []
    for s in range(sections):
        if s == sections - 1:
            current = (
                current.astype(jnp.float32) + skip_col * outs[0].astype(jnp.float32)
            ).astype(jnp.bfloat16)
        current, stored = block_forward(current, s)
        outs.append(current)
        stores.append(stored)
    grads = [None] * sections
    grad_now = cot_full
    skip_grad = None
    for s in reversed(range(sections)):
        if s == 0 and sections > 1:
            grad_now = grad_now + skip_grad
        grad_now = block_backward(grad_now, stores[s], s)
        grads[s] = grad_now
        if s == sections - 1:
            skip_grad = skip_col * grad_now
    act_keep = outs[0]
    grad_keep = grads[0]
    for s in range(1, sections):
        act_keep = jnp.where(my_phase == s, outs[s], act_keep)
        grad_keep = jnp.where(my_phase == s, grads[s], grad_keep)
    return (
        act_keep.reshape(1, chan_part, tile_dev, tile_area),
        grad_keep.reshape(1, chan_part, tile_dev, tile_area),
    )


def solution(mesh):
    placed = (
        P("ch", "tile", None),
        P("ch", "tile", None),
        P("sec", "ch", None),
        P("sec", None),
        P("sec", None, None),
        P("sec", None, None),
        P("sec", "ch"),
        P("ch"),
        P(),
        P(),
        P("tile"),
        P(),
    )
    return jax.shard_map(
        shards,
        mesh=mesh,
        in_specs=placed,
        out_specs=(P("sec", "ch", "tile", None), P("sec", "ch", "tile", None)),
        check_vma=False,
    )
```

```python
import jax
import jax.numpy as jnp
from jax import lax
from jax.sharding import PartitionSpec as P

SIDE = 32


drop_scale = 1.0 / 0.9
gelu_coeff = 0.7978845608028654
cubic_coeff = 0.044715


def mix_bits(counter):
    counter = counter * jnp.int32(739982445)
    counter = counter ^ lax.shift_right_logical(counter, jnp.int32(15))
    counter = counter * jnp.int32(695872825)
    counter = counter ^ lax.shift_right_logical(counter, jnp.int32(12))
    return counter


def keep_mask(drop_seed, section, unit_ids, pixels, hidden):
    salted = mix_bits(drop_seed + section * jnp.int32(1000003))
    counter = pixels[None, :] * jnp.int32(hidden) + unit_ids[:, None]
    mixed_bits = mix_bits(counter ^ salted)
    return (mixed_bits & jnp.int32(65535) >= jnp.int32(6554)).astype(jnp.float32)


def layer_norm(columns, norm_gain):
    centre = columns - jnp.mean(columns, axis=0, keepdims=True)
    inverse_dev = lax.rsqrt(jnp.mean(centre * centre, axis=0, keepdims=True) + 1e-06)
    normed = centre * inverse_dev
    return (normed, inverse_dev, (normed * norm_gain[:, None]).astype(jnp.bfloat16))


def norm_back(grad_in, normed, inverse_dev, norm_gain):
    scaled = grad_in * norm_gain[:, None]
    return inverse_dev * (
        scaled
        - jnp.mean(scaled, axis=0, keepdims=True)
        - normed * jnp.mean(scaled * normed, axis=0, keepdims=True)
    )


def gelu_value(pre_act):
    tanh_part = jnp.tanh(gelu_coeff * (pre_act + cubic_coeff * pre_act * pre_act * pre_act))
    return 0.5 * pre_act * (1.0 + tanh_part)


def gelu_slope(pre_act):
    tanh_part = jnp.tanh(gelu_coeff * (pre_act + cubic_coeff * pre_act * pre_act * pre_act))
    return 0.5 * (1.0 + tanh_part) + 0.5 * pre_act * (1.0 - tanh_part * tanh_part) * gelu_coeff * (
        1.0 + 3.0 * cubic_coeff * pre_act * pre_act
    )


def border_lines(grid):
    return jnp.stack([grid[:, 0, :], grid[:, -1, :], grid[:, :, 0], grid[:, :, -1]], axis=0)


def pad_tile(grid, halo):
    zero_corner = jnp.zeros(grid.shape[:1] + (1, 1), grid.dtype)
    middle = jnp.concatenate([halo[2][:, :, None], grid, halo[3][:, :, None]], axis=2)
    top_row = jnp.concatenate([zero_corner, halo[0][:, None, :], zero_corner], axis=2)
    bottom_row = jnp.concatenate([zero_corner, halo[1][:, None, :], zero_corner], axis=2)
    return jnp.concatenate([top_row, middle, bottom_row], axis=1)


def depthwise(padded, depth_kernel):
    side_len = padded.shape[1] - 2
    running = jnp.zeros(padded.shape[:1] + (side_len, side_len), jnp.float32)
    for down_step in range(3):
        for right_step in range(3):
            weight_now = depth_kernel[:, down_step * 3 + right_step][:, None, None]
            running = running + weight_now * padded[
                :, down_step : down_step + side_len, right_step : right_step + side_len
            ].astype(jnp.float32)
    return running


def depth_back(grad_in, depth_kernel):
    side_len = grad_in.shape[1]
    widened = jnp.pad(grad_in, ((0, 0), (2, 2), (2, 2)))
    running = jnp.zeros(grad_in.shape[:1] + (side_len + 2, side_len + 2), jnp.float32)
    for down_step in range(3):
        for right_step in range(3):
            weight_now = depth_kernel[:, down_step * 3 + right_step][:, None, None]
            running = running + weight_now * widened[
                :,
                2 - down_step : 4 - down_step + side_len,
                2 - right_step : 4 - right_step + side_len,
            ]
    return running


def halo_parts(padded):
    return jnp.stack(
        [padded[:, 0, 1:-1], padded[:, -1, 1:-1], padded[:, 1:-1, 0], padded[:, 1:-1, -1]], axis=0
    )


def add_border(interior, border):
    last = interior.shape[1] - 1
    top = jnp.pad(border[0][:, None, :], ((0, 0), (0, last), (0, 0)))
    bottom = jnp.pad(border[1][:, None, :], ((0, 0), (last, 0), (0, 0)))
    left = jnp.pad(border[2][:, :, None], ((0, 0), (0, 0), (0, last)))
    right = jnp.pad(border[3][:, :, None], ((0, 0), (0, 0), (last, 0)))
    return interior + top + bottom + left + right


def shards(
    fields,
    cotangent,
    depth_kernel,
    norm_gain,
    up_weight,
    down_weight,
    layer_scale,
    skip_scale,
    neighbours,
    edge_codes,
    offsets,
    drop_seed,
):
    chan_part, tile_dev, tile_area = fields.shape
    assert tile_dev == 1
    side_len = SIDE
    my_phase = lax.axis_index("sec")
    sections = lax.axis_size("sec")
    ch_index = lax.axis_index("ch")
    ch_count = lax.axis_size("ch")
    tile_count = lax.axis_size("tile")
    my_tile = lax.axis_index("tile")
    hidden = up_weight.shape[2]
    pix_part = tile_area // ch_count

    small = jnp.concatenate([depth_kernel[0].reshape(-1), norm_gain[0], layer_scale[0]])
    small_len = small.shape[0]
    high = lax.reduce_precision(small, exponent_bits=8, mantissa_bits=7)
    rest = small - high
    middle = lax.reduce_precision(rest, exponent_bits=8, mantissa_bits=7)
    low = lax.reduce_precision(rest - middle, exponent_bits=8, mantissa_bits=7)
    parts = jnp.concatenate([high, middle, low]).astype(jnp.bfloat16)
    packed = jnp.concatenate([parts, up_weight[0].reshape(-1), down_weight[0].reshape(-1)])
    packed_got = [packed]
    for shift in range(1, sections):
        route_now = [(i, (i + shift) % sections) for i in range(sections)]
        packed_got.append(lax.ppermute(packed, "sec", route_now))

    def section_weights(s):
        behind = (my_phase - s) % sections
        got = packed_got[0]
        for shift in range(1, sections):
            got = jnp.where(behind == shift, packed_got[shift], got)
        small_s = (
            got[:small_len].astype(jnp.float32) + got[small_len : 2 * small_len].astype(jnp.float32)
        ) + got[2 * small_len : 3 * small_len].astype(jnp.float32)
        large_s = got[3 * small_len :]
        dk_len = chan_part * 9
        cut = up_weight.shape[1] * hidden
        return (
            small_s[:dk_len].reshape(chan_part, 9),
            small_s[dk_len : dk_len + norm_gain.shape[1]],
            small_s[dk_len + norm_gain.shape[1] :],
            large_s[:cut].reshape(up_weight.shape[1:]),
            large_s[cut:].reshape(down_weight.shape[1:]),
        )

    dk_all, gain_all, scale_all, up_all, down_all = [], [], [], [], []
    for s in range(sections):
        for store, part in zip((dk_all, gain_all, scale_all, up_all, down_all), section_weights(s)):
            store.append(part)

    side_code = edge_codes % 4
    own_flip = edge_codes[my_tile] >= 4
    line_ids = jnp.arange(4, dtype=jnp.int32)
    same_tile = neighbours[:, :, None] == neighbours[:, None, :]
    earlier = line_ids[None, :] < line_ids[:, None]
    rank = jnp.sum((same_tile & earlier[None]).astype(jnp.int32), axis=2)
    narrow = jnp.max(rank) < 2

    def send_pick(width):
        hit = (
            (neighbours == my_tile)[:, :, None, None]
            & (rank[:, :, None, None] == jnp.arange(width, dtype=jnp.int32)[None, None, :, None])
            & (side_code[:, :, None, None] == line_ids[None, None, None, :])
        )
        return jnp.sum(hit.astype(jnp.float32), axis=1).astype(jnp.bfloat16)

    def take_pick(width):
        hit = (
            neighbours[my_tile][:, None, None]
            == jnp.arange(tile_count, dtype=jnp.int32)[None, :, None]
        ) & (rank[my_tile][:, None, None] == jnp.arange(width, dtype=jnp.int32)[None, None, :])
        return hit.astype(jnp.bfloat16)

    pixel_ids = offsets[0] + ch_index * pix_part + jnp.arange(pix_part, dtype=jnp.int32)
    unit_ids = jnp.arange(hidden, dtype=jnp.int32)

    def route_with(width):
        pick = send_pick(width)
        take = take_pick(width)

        def run(lines):
            send = jnp.einsum("jrk,kcs->jrcs", pick, lines, preferred_element_type=jnp.float32)
            send = send.astype(jnp.bfloat16).reshape(tile_count, -1)
            got = lax.all_to_all(send, "tile", 0, 0, tiled=True)
            got = got.reshape(tile_count, width, chan_part, side_len)
            return jnp.einsum("esr,srcx->ecx", take, got, preferred_element_type=jnp.float32)

        return run

    route_narrow = route_with(2)
    route_wide = route_with(4)

    def route(lines):
        return lax.cond(narrow, route_narrow, route_wide, lines)

    def ch_exchange(pieces):
        sent = [lax.dynamic_index_in_dim(pieces, ch_index, 0, keepdims=False)]
        for shift in range(1, ch_count):
            piece = lax.dynamic_index_in_dim(pieces, (ch_index + shift) % ch_count, 0, keepdims=False)
            pairs = [(k, (k + shift) % ch_count) for k in range(ch_count)]
            sent.append(lax.ppermute(piece, "ch", pairs))
        by_shift = jnp.stack(sent)
        sources = (ch_index - jnp.arange(ch_count, dtype=jnp.int32)) % ch_count
        return jnp.take(by_shift, sources, axis=0)

    def to_pixels(block):
        rows = block.shape[0]
        pieces = block.reshape(rows, ch_count, pix_part).transpose(1, 0, 2)
        return ch_exchange(pieces).reshape(rows * ch_count, pix_part)

    def to_channels(block):
        pieces = block.reshape(ch_count, chan_part, pix_part)
        return ch_exchange(pieces).transpose(1, 0, 2).reshape(chan_part, tile_area)

    def block_forward(block_in, s):
        grid = block_in.reshape(chan_part, side_len, side_len)
        halo = route(border_lines(grid)).astype(jnp.bfloat16)
        halo = jnp.where(own_flip[:, None, None], halo[..., ::-1], halo)
        mixed = depthwise(pad_tile(grid, halo), dk_all[s]).astype(jnp.bfloat16)
        mixed = mixed.reshape(chan_part, tile_area)
        if s == 0:
            both = to_pixels(jnp.concatenate([mixed, last_scaled], axis=0).reshape(2 * chan_part, tile_area))
            both = both.reshape(ch_count, 2, chan_part, pix_part)
            cols = both[:, 0].reshape(-1, pix_part)
            early_cols.append(both[:, 1].reshape(-1, pix_part))
        else:
            cols = to_pixels(mixed)
        normed, inverse_dev, scaled_in = layer_norm(cols.astype(jnp.float32), gain_all[s])
        pre_act = jnp.einsum("ch,cp->hp", up_all[s], scaled_in, preferred_element_type=jnp.float32)
        keeper = keep_mask(drop_seed, s, unit_ids, pixel_ids, hidden)
        dropped = (gelu_value(pre_act) * keeper * drop_scale).astype(jnp.bfloat16)
        branch = jnp.einsum("hc,hp->cp", down_all[s], dropped, preferred_element_type=jnp.float32)
        branch = to_channels(branch)
        out = (
            block_in.astype(jnp.float32) + scale_all[s][:, None] * branch
        ).astype(jnp.bfloat16)
        return out, (normed, inverse_dev, pre_act, keeper)

    def block_backward(grad_out, stored, s):
        normed, inverse_dev, pre_act, keeper = stored
        if s == sections - 1:
            cols = early_cols[0]
        else:
            scaled_grad = (scale_all[s][:, None] * grad_out).astype(jnp.bfloat16)
            cols = to_pixels(scaled_grad)
        grad_drop = jnp.einsum("hc,cp->hp", down_all[s], cols, preferred_element_type=jnp.float32)
        grad_pre = (grad_drop * keeper * drop_scale * gelu_slope(pre_act)).astype(jnp.bfloat16)
        grad_norm = jnp.einsum("ch,hp->cp", up_all[s], grad_pre, preferred_element_type=jnp.float32)
        grad_mixed = norm_back(grad_norm, normed, inverse_dev, gain_all[s])
        grad_mixed = to_channels(grad_mixed).reshape(chan_part, side_len, side_len)
        grad_padded = depth_back(grad_mixed, dk_all[s])
        edge_grad = halo_parts(grad_padded)
        edge_grad = jnp.where(own_flip[:, None, None], edge_grad[..., ::-1], edge_grad).astype(
            jnp.bfloat16
        )
        routed = route(edge_grad)
        interior = add_border(grad_padded[:, 1:-1, 1:-1], routed)
        return grad_out + interior.reshape(chan_part, tile_area)

    skip_col = skip_scale[:, None]
    cot_full = cotangent.reshape(chan_part, tile_area).astype(jnp.float32)
    last_scaled = (scale_all[sections - 1][:, None] * cot_full).astype(jnp.bfloat16)
    early_cols = []
    current = fields.reshape(chan_part, tile_area)
    outs = []
    stores = []
    for s in range(sections):
        if s == sections - 1:
            current = (
                current.astype(jnp.float32) + skip_col * outs[0].astype(jnp.float32)
            ).astype(jnp.bfloat16)
        current, stored = block_forward(current, s)
        outs.append(current)
        stores.append(stored)
    grads = [None] * sections
    grad_now = cot_full
    skip_grad = None
    for s in reversed(range(sections)):
        if s == 0 and sections > 1:
            grad_now = grad_now + skip_grad
        grad_now = block_backward(grad_now, stores[s], s)
        grads[s] = grad_now
        if s == sections - 1:
            skip_grad = skip_col * grad_now
    act_keep = outs[0]
    grad_keep = grads[0]
    for s in range(1, sections):
        act_keep = jnp.where(my_phase == s, outs[s], act_keep)
        grad_keep = jnp.where(my_phase == s, grads[s], grad_keep)
    return (
        act_keep.reshape(1, chan_part, tile_dev, tile_area),
        grad_keep.reshape(1, chan_part, tile_dev, tile_area),
    )


def solution(mesh):
    placed = (
        P("ch", "tile", None),
        P("ch", "tile", None),
        P("sec", "ch", None),
        P("sec", None),
        P("sec", None, None),
        P("sec", None, None),
        P("sec", "ch"),
        P("ch"),
        P(),
        P(),
        P("tile"),
        P(),
    )
    return jax.shard_map(
        shards,
        mesh=mesh,
        in_specs=placed,
        out_specs=(P("sec", "ch", "tile", None), P("sec", "ch", "tile", None)),
        check_vma=False,
    )
```

```python
import jax
import jax.numpy as jnp
from jax import lax
from jax.sharding import PartitionSpec as P

SIDE = 32


drop_scale = 1.0 / 0.9
gelu_coeff = 0.7978845608028654
cubic_coeff = 0.044715


def mix_bits(counter):
    counter = counter * jnp.int32(739982445)
    counter = counter ^ lax.shift_right_logical(counter, jnp.int32(15))
    counter = counter * jnp.int32(695872825)
    counter = counter ^ lax.shift_right_logical(counter, jnp.int32(12))
    return counter


def keep_mask(drop_seed, section, unit_ids, pixels, hidden):
    salted = mix_bits(drop_seed + section * jnp.int32(1000003))
    counter = pixels[None, :] * jnp.int32(hidden) + unit_ids[:, None]
    mixed_bits = mix_bits(counter ^ salted)
    return (mixed_bits & jnp.int32(65535) >= jnp.int32(6554)).astype(jnp.float32)


def layer_norm(columns, norm_gain):
    centre = columns - jnp.mean(columns, axis=0, keepdims=True)
    inverse_dev = lax.rsqrt(jnp.mean(centre * centre, axis=0, keepdims=True) + 1e-06)
    normed = centre * inverse_dev
    return (normed, inverse_dev, (normed * norm_gain[:, None]).astype(jnp.bfloat16))


def norm_back(grad_in, normed, inverse_dev, norm_gain):
    scaled = grad_in * norm_gain[:, None]
    return inverse_dev * (
        scaled
        - jnp.mean(scaled, axis=0, keepdims=True)
        - normed * jnp.mean(scaled * normed, axis=0, keepdims=True)
    )


def gelu_value(pre_act):
    tanh_part = jnp.tanh(gelu_coeff * (pre_act + cubic_coeff * pre_act * pre_act * pre_act))
    return 0.5 * pre_act * (1.0 + tanh_part)


def gelu_slope(pre_act):
    tanh_part = jnp.tanh(gelu_coeff * (pre_act + cubic_coeff * pre_act * pre_act * pre_act))
    return 0.5 * (1.0 + tanh_part) + 0.5 * pre_act * (1.0 - tanh_part * tanh_part) * gelu_coeff * (
        1.0 + 3.0 * cubic_coeff * pre_act * pre_act
    )


def border_lines(grid):
    return jnp.stack([grid[:, 0, :], grid[:, -1, :], grid[:, :, 0], grid[:, :, -1]], axis=0)


def pad_tile(grid, halo):
    zero_corner = jnp.zeros(grid.shape[:1] + (1, 1), grid.dtype)
    middle = jnp.concatenate([halo[2][:, :, None], grid, halo[3][:, :, None]], axis=2)
    top_row = jnp.concatenate([zero_corner, halo[0][:, None, :], zero_corner], axis=2)
    bottom_row = jnp.concatenate([zero_corner, halo[1][:, None, :], zero_corner], axis=2)
    return jnp.concatenate([top_row, middle, bottom_row], axis=1)


def depthwise(padded, depth_kernel):
    side_len = padded.shape[1] - 2
    running = jnp.zeros(padded.shape[:1] + (side_len, side_len), jnp.float32)
    for down_step in range(3):
        for right_step in range(3):
            weight_now = depth_kernel[:, down_step * 3 + right_step][:, None, None]
            running = running + weight_now * padded[
                :, down_step : down_step + side_len, right_step : right_step + side_len
            ].astype(jnp.float32)
    return running


def depth_back(grad_in, depth_kernel):
    side_len = grad_in.shape[1]
    widened = jnp.pad(grad_in, ((0, 0), (2, 2), (2, 2)))
    running = jnp.zeros(grad_in.shape[:1] + (side_len + 2, side_len + 2), jnp.float32)
    for down_step in range(3):
        for right_step in range(3):
            weight_now = depth_kernel[:, down_step * 3 + right_step][:, None, None]
            running = running + weight_now * widened[
                :,
                2 - down_step : 4 - down_step + side_len,
                2 - right_step : 4 - right_step + side_len,
            ]
    return running


def halo_parts(padded):
    return jnp.stack(
        [padded[:, 0, 1:-1], padded[:, -1, 1:-1], padded[:, 1:-1, 0], padded[:, 1:-1, -1]], axis=0
    )


def add_border(interior, border):
    last = interior.shape[1] - 1
    top = jnp.pad(border[0][:, None, :], ((0, 0), (0, last), (0, 0)))
    bottom = jnp.pad(border[1][:, None, :], ((0, 0), (last, 0), (0, 0)))
    left = jnp.pad(border[2][:, :, None], ((0, 0), (0, 0), (0, last)))
    right = jnp.pad(border[3][:, :, None], ((0, 0), (0, 0), (last, 0)))
    return interior + top + bottom + left + right


def shards(
    fields,
    cotangent,
    depth_kernel,
    norm_gain,
    up_weight,
    down_weight,
    layer_scale,
    skip_scale,
    neighbours,
    edge_codes,
    offsets,
    drop_seed,
):
    chan_part, tile_dev, tile_area = fields.shape
    assert tile_dev == 1
    side_len = SIDE
    my_phase = lax.axis_index("sec")
    sections = lax.axis_size("sec")
    ch_index = lax.axis_index("ch")
    ch_count = lax.axis_size("ch")
    tile_count = lax.axis_size("tile")
    my_tile = lax.axis_index("tile")
    hidden = up_weight.shape[2]
    pix_part = tile_area // ch_count

    small = jnp.concatenate([depth_kernel[0].reshape(-1), norm_gain[0], layer_scale[0]])
    small_len = small.shape[0]
    high = lax.reduce_precision(small, exponent_bits=8, mantissa_bits=7)
    rest = small - high
    middle = lax.reduce_precision(rest, exponent_bits=8, mantissa_bits=7)
    low = lax.reduce_precision(rest - middle, exponent_bits=8, mantissa_bits=7)
    parts = jnp.concatenate([high, middle, low]).astype(jnp.bfloat16)
    packed = jnp.concatenate([parts, up_weight[0].reshape(-1), down_weight[0].reshape(-1)])
    packed_got = [packed]
    for shift in range(1, sections):
        route_now = [(i, (i + shift) % sections) for i in range(sections)]
        packed_got.append(lax.ppermute(packed, "sec", route_now))

    def section_weights(s):
        behind = (my_phase - s) % sections
        got = packed_got[0]
        for shift in range(1, sections):
            got = jnp.where(behind == shift, packed_got[shift], got)
        small_s = (
            got[:small_len].astype(jnp.float32) + got[small_len : 2 * small_len].astype(jnp.float32)
        ) + got[2 * small_len : 3 * small_len].astype(jnp.float32)
        large_s = got[3 * small_len :]
        dk_len = chan_part * 9
        cut = up_weight.shape[1] * hidden
        return (
            small_s[:dk_len].reshape(chan_part, 9),
            small_s[dk_len : dk_len + norm_gain.shape[1]],
            small_s[dk_len + norm_gain.shape[1] :],
            large_s[:cut].reshape(up_weight.shape[1:]),
            large_s[cut:].reshape(down_weight.shape[1:]),
        )

    dk_all, gain_all, scale_all, up_all, down_all = [], [], [], [], []
    for s in range(sections):
        for store, part in zip((dk_all, gain_all, scale_all, up_all, down_all), section_weights(s)):
            store.append(part)

    side_code = edge_codes % 4
    own_flip = edge_codes[my_tile] >= 4
    line_ids = jnp.arange(4, dtype=jnp.int32)
    same_tile = neighbours[:, :, None] == neighbours[:, None, :]
    earlier = line_ids[None, :] < line_ids[:, None]
    rank = jnp.sum((same_tile & earlier[None]).astype(jnp.int32), axis=2)
    narrow = jnp.max(rank) < 2

    def send_pick(width):
        hit = (
            (neighbours == my_tile)[:, :, None, None]
            & (rank[:, :, None, None] == jnp.arange(width, dtype=jnp.int32)[None, None, :, None])
            & (side_code[:, :, None, None] == line_ids[None, None, None, :])
        )
        return jnp.sum(hit.astype(jnp.float32), axis=1).astype(jnp.bfloat16)

    def take_pick(width):
        hit = (
            neighbours[my_tile][:, None, None]
            == jnp.arange(tile_count, dtype=jnp.int32)[None, :, None]
        ) & (rank[my_tile][:, None, None] == jnp.arange(width, dtype=jnp.int32)[None, None, :])
        return hit.astype(jnp.bfloat16)

    pixel_ids = offsets[0] + ch_index * pix_part + jnp.arange(pix_part, dtype=jnp.int32)
    unit_ids = jnp.arange(hidden, dtype=jnp.int32)

    def route_with(width):
        pick = send_pick(width)
        take = take_pick(width)

        def run(lines):
            send = jnp.einsum("jrk,kcs->jrcs", pick, lines, preferred_element_type=jnp.float32)
            send = send.astype(jnp.bfloat16).reshape(tile_count, -1)
            got = lax.all_to_all(send, "tile", 0, 0, tiled=True)
            got = got.reshape(tile_count, width, chan_part, side_len)
            return jnp.einsum("esr,srcx->ecx", take, got, preferred_element_type=jnp.float32)

        return run

    route_narrow = route_with(2)
    route_wide = route_with(4)

    def route(lines):
        return lax.cond(narrow, route_narrow, route_wide, lines)

    def to_pixels(block):
        return lax.all_to_all(block, "ch", 1, 0, tiled=True)

    def to_channels(block):
        return lax.all_to_all(block, "ch", 0, 1, tiled=True)

    skip_col = skip_scale[:, None]
    cot_full = cotangent.reshape(chan_part, tile_area).astype(jnp.float32)
    last_scaled = (scale_all[sections - 1][:, None] * cot_full).astype(jnp.bfloat16)
    weight_stack = tuple(jnp.stack(w) for w in (dk_all, gain_all, scale_all, up_all, down_all))
    section_ids = jnp.arange(sections, dtype=jnp.int32)

    def forward_step(carry, xs):
        current, encoded = carry
        kernel, gain, scale, up, down, s = xs
        joined = (current.astype(jnp.float32) + skip_col * encoded.astype(jnp.float32)).astype(
            jnp.bfloat16
        )
        block_in = jnp.where(s == sections - 1, joined, current)
        grid = block_in.reshape(chan_part, side_len, side_len)
        halo = route(border_lines(grid)).astype(jnp.bfloat16)
        halo = jnp.where(own_flip[:, None, None], halo[..., ::-1], halo)
        mixed = depthwise(pad_tile(grid, halo), kernel).astype(jnp.bfloat16)
        mixed = mixed.reshape(chan_part, tile_area)
        both = jnp.stack([mixed, last_scaled]).reshape(2, chan_part, ch_count, pix_part)
        both = lax.all_to_all(both, "ch", 2, 1, tiled=True)
        cols = both[0].reshape(-1, pix_part)
        early = both[1].reshape(-1, pix_part)
        normed, inverse_dev, scaled_in = layer_norm(cols.astype(jnp.float32), gain)
        pre_act = jnp.einsum("ch,cp->hp", up, scaled_in, preferred_element_type=jnp.float32)
        keeper = keep_mask(drop_seed, s, unit_ids, pixel_ids, hidden)
        dropped = (gelu_value(pre_act) * keeper * drop_scale).astype(jnp.bfloat16)
        branch = jnp.einsum("hc,hp->cp", down, dropped, preferred_element_type=jnp.float32)
        branch = to_channels(branch)
        out = (block_in.astype(jnp.float32) + scale[:, None] * branch).astype(jnp.bfloat16)
        encoded = jnp.where(s == 0, out, encoded)
        return (out, encoded), (out, normed, inverse_dev, pre_act, keeper, early)

    start_state = fields.reshape(chan_part, tile_area)
    _, (outs, *stored) = lax.scan(
        forward_step, (start_state, start_state), weight_stack + (section_ids,)
    )
    early_cols = stored.pop()[0]

    def backward_step(carry, xs):
        grad_now, skip_grad = carry
        kernel, gain, scale, up, down, s, normed, inverse_dev, pre_act, keeper = xs
        grad_out = jnp.where(s == 0, grad_now + skip_grad, grad_now)
        cols = lax.cond(
            s == sections - 1,
            lambda g: early_cols,
            lambda g: to_pixels((scale[:, None] * g).astype(jnp.bfloat16)),
            grad_out,
        )
        grad_drop = jnp.einsum("hc,cp->hp", down, cols, preferred_element_type=jnp.float32)
        grad_pre = (grad_drop * keeper * drop_scale * gelu_slope(pre_act)).astype(jnp.bfloat16)
        grad_norm = jnp.einsum("ch,hp->cp", up, grad_pre, preferred_element_type=jnp.float32)
        grad_mixed = norm_back(grad_norm, normed, inverse_dev, gain)
        grad_mixed = to_channels(grad_mixed).reshape(chan_part, side_len, side_len)
        grad_padded = depth_back(grad_mixed, kernel)
        edge_grad = halo_parts(grad_padded)
        edge_grad = jnp.where(own_flip[:, None, None], edge_grad[..., ::-1], edge_grad).astype(
            jnp.bfloat16
        )
        routed = route(edge_grad)
        interior = add_border(grad_padded[:, 1:-1, 1:-1], routed)
        grad_in = grad_out + interior.reshape(chan_part, tile_area)
        skip_grad = jnp.where(s == sections - 1, skip_col * grad_in, skip_grad)
        return (grad_in, skip_grad), grad_in

    _, grads = lax.scan(
        backward_step,
        (cot_full, jnp.zeros_like(cot_full)),
        weight_stack + (section_ids,) + tuple(stored),
        reverse=True,
    )
    act_keep = lax.dynamic_index_in_dim(outs, my_phase, 0, keepdims=False)
    grad_keep = lax.dynamic_index_in_dim(grads, my_phase, 0, keepdims=False)
    return (
        act_keep.reshape(1, chan_part, tile_dev, tile_area),
        grad_keep.reshape(1, chan_part, tile_dev, tile_area),
    )


def solution(mesh):
    placed = (
        P("ch", "tile", None),
        P("ch", "tile", None),
        P("sec", "ch", None),
        P("sec", None),
        P("sec", None, None),
        P("sec", None, None),
        P("sec", "ch"),
        P("ch"),
        P(),
        P(),
        P("tile"),
        P(),
    )
    return jax.shard_map(
        shards,
        mesh=mesh,
        in_specs=placed,
        out_specs=(P("sec", "ch", "tile", None), P("sec", "ch", "tile", None)),
        check_vma=False,
    )
```

```python
import jax
import jax.numpy as jnp
from jax import lax
from jax.sharding import PartitionSpec as P

SIDE = 32


drop_scale = 1.0 / 0.9
gelu_coeff = 0.7978845608028654
cubic_coeff = 0.044715


def mix_bits(counter):
    counter = counter * jnp.int32(739982445)
    counter = counter ^ lax.shift_right_logical(counter, jnp.int32(15))
    counter = counter * jnp.int32(695872825)
    counter = counter ^ lax.shift_right_logical(counter, jnp.int32(12))
    return counter


def keep_mask(drop_seed, section, unit_ids, pixels, hidden):
    salted = mix_bits(drop_seed + section * jnp.int32(1000003))
    counter = pixels[None, :] * jnp.int32(hidden) + unit_ids[:, None]
    mixed_bits = mix_bits(counter ^ salted)
    return (mixed_bits & jnp.int32(65535) >= jnp.int32(6554)).astype(jnp.float32)


def layer_norm(columns, norm_gain):
    centre = columns - jnp.mean(columns, axis=0, keepdims=True)
    inverse_dev = lax.rsqrt(jnp.mean(centre * centre, axis=0, keepdims=True) + 1e-06)
    normed = centre * inverse_dev
    return (normed, inverse_dev, (normed * norm_gain[:, None]).astype(jnp.bfloat16))


def norm_back(grad_in, normed, inverse_dev, norm_gain):
    scaled = grad_in * norm_gain[:, None]
    return inverse_dev * (
        scaled
        - jnp.mean(scaled, axis=0, keepdims=True)
        - normed * jnp.mean(scaled * normed, axis=0, keepdims=True)
    )


def gelu_value(pre_act):
    tanh_part = jnp.tanh(gelu_coeff * (pre_act + cubic_coeff * pre_act * pre_act * pre_act))
    return 0.5 * pre_act * (1.0 + tanh_part)


def gelu_slope(pre_act):
    tanh_part = jnp.tanh(gelu_coeff * (pre_act + cubic_coeff * pre_act * pre_act * pre_act))
    return 0.5 * (1.0 + tanh_part) + 0.5 * pre_act * (1.0 - tanh_part * tanh_part) * gelu_coeff * (
        1.0 + 3.0 * cubic_coeff * pre_act * pre_act
    )


def border_lines(grid):
    return jnp.stack([grid[:, 0, :], grid[:, -1, :], grid[:, :, 0], grid[:, :, -1]], axis=0)


def pad_tile(grid, halo):
    zero_corner = jnp.zeros(grid.shape[:1] + (1, 1), grid.dtype)
    middle = jnp.concatenate([halo[2][:, :, None], grid, halo[3][:, :, None]], axis=2)
    top_row = jnp.concatenate([zero_corner, halo[0][:, None, :], zero_corner], axis=2)
    bottom_row = jnp.concatenate([zero_corner, halo[1][:, None, :], zero_corner], axis=2)
    return jnp.concatenate([top_row, middle, bottom_row], axis=1)


def depthwise(padded, depth_kernel):
    side_len = padded.shape[1] - 2
    running = jnp.zeros(padded.shape[:1] + (side_len, side_len), jnp.float32)
    for down_step in range(3):
        for right_step in range(3):
            weight_now = depth_kernel[:, down_step * 3 + right_step][:, None, None]
            running = running + weight_now * padded[
                :, down_step : down_step + side_len, right_step : right_step + side_len
            ].astype(jnp.float32)
    return running


def depth_back(grad_in, depth_kernel):
    side_len = grad_in.shape[1]
    widened = jnp.pad(grad_in, ((0, 0), (2, 2), (2, 2)))
    running = jnp.zeros(grad_in.shape[:1] + (side_len + 2, side_len + 2), jnp.float32)
    for down_step in range(3):
        for right_step in range(3):
            weight_now = depth_kernel[:, down_step * 3 + right_step][:, None, None]
            running = running + weight_now * widened[
                :,
                2 - down_step : 4 - down_step + side_len,
                2 - right_step : 4 - right_step + side_len,
            ]
    return running


def halo_parts(padded):
    return jnp.stack(
        [padded[:, 0, 1:-1], padded[:, -1, 1:-1], padded[:, 1:-1, 0], padded[:, 1:-1, -1]], axis=0
    )


def add_border(interior, border):
    last = interior.shape[1] - 1
    top = jnp.pad(border[0][:, None, :], ((0, 0), (0, last), (0, 0)))
    bottom = jnp.pad(border[1][:, None, :], ((0, 0), (last, 0), (0, 0)))
    left = jnp.pad(border[2][:, :, None], ((0, 0), (0, 0), (0, last)))
    right = jnp.pad(border[3][:, :, None], ((0, 0), (0, 0), (last, 0)))
    return interior + top + bottom + left + right


def shards(
    fields,
    cotangent,
    depth_kernel,
    norm_gain,
    up_weight,
    down_weight,
    layer_scale,
    skip_scale,
    neighbours,
    edge_codes,
    offsets,
    drop_seed,
):
    chan_part, tile_dev, tile_area = fields.shape
    assert tile_dev == 1
    side_len = SIDE
    my_phase = lax.axis_index("sec")
    sections = lax.axis_size("sec")
    ch_index = lax.axis_index("ch")
    ch_count = lax.axis_size("ch")
    tile_count = lax.axis_size("tile")
    my_tile = lax.axis_index("tile")
    hidden = up_weight.shape[2]
    pix_part = tile_area // ch_count

    small = jnp.concatenate([depth_kernel[0].reshape(-1), norm_gain[0], layer_scale[0]])
    small_len = small.shape[0]
    high = lax.reduce_precision(small, exponent_bits=8, mantissa_bits=7)
    rest = small - high
    middle = lax.reduce_precision(rest, exponent_bits=8, mantissa_bits=7)
    low = lax.reduce_precision(rest - middle, exponent_bits=8, mantissa_bits=7)
    parts = jnp.concatenate([high, middle, low]).astype(jnp.bfloat16)
    packed = jnp.concatenate([parts, up_weight[0].reshape(-1), down_weight[0].reshape(-1)])
    packed_got = [packed]
    for shift in range(1, sections):
        route_now = [(i, (i + shift) % sections) for i in range(sections)]
        packed_got.append(lax.ppermute(packed, "sec", route_now))

    def section_weights(s):
        behind = (my_phase - s) % sections
        got = packed_got[0]
        for shift in range(1, sections):
            got = jnp.where(behind == shift, packed_got[shift], got)
        small_s = (
            got[:small_len].astype(jnp.float32) + got[small_len : 2 * small_len].astype(jnp.float32)
        ) + got[2 * small_len : 3 * small_len].astype(jnp.float32)
        large_s = got[3 * small_len :]
        dk_len = chan_part * 9
        cut = up_weight.shape[1] * hidden
        return (
            small_s[:dk_len].reshape(chan_part, 9),
            small_s[dk_len : dk_len + norm_gain.shape[1]],
            small_s[dk_len + norm_gain.shape[1] :],
            large_s[:cut].reshape(up_weight.shape[1:]),
            large_s[cut:].reshape(down_weight.shape[1:]),
        )

    dk_all, gain_all, scale_all, up_all, down_all = [], [], [], [], []
    for s in range(sections):
        for store, part in zip((dk_all, gain_all, scale_all, up_all, down_all), section_weights(s)):
            store.append(part)

    side_code = edge_codes % 4
    own_flip = edge_codes[my_tile] >= 4
    line_ids = jnp.arange(4, dtype=jnp.int32)
    same_tile = neighbours[:, :, None] == neighbours[:, None, :]
    earlier = line_ids[None, :] < line_ids[:, None]
    rank = jnp.sum((same_tile & earlier[None]).astype(jnp.int32), axis=2)
    narrow = jnp.max(rank) < 2

    def send_pick(width):
        hit = (
            (neighbours == my_tile)[:, :, None, None]
            & (rank[:, :, None, None] == jnp.arange(width, dtype=jnp.int32)[None, None, :, None])
            & (side_code[:, :, None, None] == line_ids[None, None, None, :])
        )
        return jnp.sum(hit.astype(jnp.float32), axis=1).astype(jnp.bfloat16)

    def take_pick(width):
        hit = (
            neighbours[my_tile][:, None, None]
            == jnp.arange(tile_count, dtype=jnp.int32)[None, :, None]
        ) & (rank[my_tile][:, None, None] == jnp.arange(width, dtype=jnp.int32)[None, None, :])
        return hit.astype(jnp.bfloat16)

    pixel_ids = offsets[0] + ch_index * pix_part + jnp.arange(pix_part, dtype=jnp.int32)
    unit_ids = jnp.arange(hidden, dtype=jnp.int32)

    def route_with(width):
        pick = send_pick(width)
        take = take_pick(width)

        def run(lines):
            send = jnp.einsum("jrk,kcs->jrcs", pick, lines, preferred_element_type=jnp.float32)
            send = send.astype(jnp.bfloat16).reshape(tile_count, -1)
            got = lax.all_to_all(send, "tile", 0, 0, tiled=True)
            got = got.reshape(tile_count, width, chan_part, side_len)
            return jnp.einsum("esr,srcx->ecx", take, got, preferred_element_type=jnp.float32)

        return run

    route_narrow = route_with(2)
    route_wide = route_with(4)

    def route(lines):
        return lax.cond(narrow, route_narrow, route_wide, lines)

    def to_pixels(block):
        return lax.all_to_all(block, "ch", 1, 0, tiled=True)

    def to_channels(block):
        return lax.all_to_all(block, "ch", 0, 1, tiled=True)

    def block_forward(block_in, s):
        grid = block_in.reshape(chan_part, side_len, side_len)
        halo = route(border_lines(grid)).astype(jnp.bfloat16)
        halo = jnp.where(own_flip[:, None, None], halo[..., ::-1], halo)
        mixed = depthwise(pad_tile(grid, halo), dk_all[s]).astype(jnp.bfloat16)
        mixed = mixed.reshape(chan_part, tile_area)
        if s == 0:
            both = jnp.stack([mixed, last_scaled]).reshape(2, chan_part, ch_count, pix_part)
            both = lax.all_to_all(both, "ch", 2, 1, tiled=True)
            cols = both[0].reshape(-1, pix_part)
            early_cols.append(both[1].reshape(-1, pix_part))
        else:
            cols = to_pixels(mixed)
        normed, inverse_dev, scaled_in = layer_norm(cols.astype(jnp.float32), gain_all[s])
        pre_act = jnp.einsum("ch,cp->hp", up_all[s], scaled_in, preferred_element_type=jnp.float32)
        keeper = keep_mask(drop_seed, s, unit_ids, pixel_ids, hidden)
        dropped = (gelu_value(pre_act) * keeper * drop_scale).astype(jnp.bfloat16)
        branch = jnp.einsum("hc,hp->cp", down_all[s], dropped, preferred_element_type=jnp.float32)
        branch = to_channels(branch)
        out = (
            block_in.astype(jnp.float32) + scale_all[s][:, None] * branch
        ).astype(jnp.bfloat16)
        return out, (normed, inverse_dev, pre_act, keeper)

    skip_col = skip_scale[:, None]
    cot_full = cotangent.reshape(chan_part, tile_area).astype(jnp.float32)
    last_scaled = (scale_all[sections - 1][:, None] * cot_full).astype(jnp.bfloat16)
    early_cols = []
    current = fields.reshape(chan_part, tile_area)
    outs = []
    stores = []
    for s in range(sections):
        if s == sections - 1:
            current = (
                current.astype(jnp.float32) + skip_col * outs[0].astype(jnp.float32)
            ).astype(jnp.bfloat16)
        current, stored = block_forward(current, s)
        outs.append(current)
        stores.append(stored)
    weight_stack = tuple(jnp.stack(w) for w in (dk_all, gain_all, scale_all, up_all, down_all))
    stored_stack = tuple(jnp.stack(part) for part in zip(*stores))
    section_ids = jnp.arange(sections, dtype=jnp.int32)
    early = early_cols[0]

    def backward_step(carry, xs):
        grad_now, skip_grad = carry
        kernel, gain, scale, up, down, s, normed, inverse_dev, pre_act, keeper = xs
        grad_out = jnp.where(s == 0, grad_now + skip_grad, grad_now)
        cols = lax.cond(
            s == sections - 1,
            lambda g: early,
            lambda g: to_pixels((scale[:, None] * g).astype(jnp.bfloat16)),
            grad_out,
        )
        grad_drop = jnp.einsum("hc,cp->hp", down, cols, preferred_element_type=jnp.float32)
        grad_pre = (grad_drop * keeper * drop_scale * gelu_slope(pre_act)).astype(jnp.bfloat16)
        grad_norm = jnp.einsum("ch,hp->cp", up, grad_pre, preferred_element_type=jnp.float32)
        grad_mixed = norm_back(grad_norm, normed, inverse_dev, gain)
        grad_mixed = to_channels(grad_mixed).reshape(chan_part, side_len, side_len)
        grad_padded = depth_back(grad_mixed, kernel)
        edge_grad = halo_parts(grad_padded)
        edge_grad = jnp.where(own_flip[:, None, None], edge_grad[..., ::-1], edge_grad).astype(
            jnp.bfloat16
        )
        routed = route(edge_grad)
        interior = add_border(grad_padded[:, 1:-1, 1:-1], routed)
        grad_in = grad_out + interior.reshape(chan_part, tile_area)
        skip_grad = jnp.where(s == sections - 1, skip_col * grad_in, skip_grad)
        return (grad_in, skip_grad), grad_in

    _, grads = lax.scan(
        backward_step,
        (cot_full, jnp.zeros_like(cot_full)),
        weight_stack + (section_ids,) + stored_stack,
        reverse=True,
    )
    act_keep = outs[0]
    for s in range(1, sections):
        act_keep = jnp.where(my_phase == s, outs[s], act_keep)
    grad_keep = lax.dynamic_index_in_dim(grads, my_phase, 0, keepdims=False)
    return (
        act_keep.reshape(1, chan_part, tile_dev, tile_area),
        grad_keep.reshape(1, chan_part, tile_dev, tile_area),
    )


def solution(mesh):
    placed = (
        P("ch", "tile", None),
        P("ch", "tile", None),
        P("sec", "ch", None),
        P("sec", None),
        P("sec", None, None),
        P("sec", None, None),
        P("sec", "ch"),
        P("ch"),
        P(),
        P(),
        P("tile"),
        P(),
    )
    return jax.shard_map(
        shards,
        mesh=mesh,
        in_specs=placed,
        out_specs=(P("sec", "ch", "tile", None), P("sec", "ch", "tile", None)),
        check_vma=False,
    )
```

```python
import jax
import jax.numpy as jnp
from jax import lax
from jax.sharding import PartitionSpec as P

SIDE = 32


drop_scale = 1.0 / 0.9
gelu_coeff = 0.7978845608028654
cubic_coeff = 0.044715


def mix_bits(counter):
    counter = counter * jnp.int32(739982445)
    counter = counter ^ lax.shift_right_logical(counter, jnp.int32(15))
    counter = counter * jnp.int32(695872825)
    counter = counter ^ lax.shift_right_logical(counter, jnp.int32(12))
    return counter


def keep_mask(drop_seed, section, unit_ids, pixels, hidden):
    salted = mix_bits(drop_seed + section * jnp.int32(1000003))
    counter = pixels[None, :] * jnp.int32(hidden) + unit_ids[:, None]
    mixed_bits = mix_bits(counter ^ salted)
    return (mixed_bits & jnp.int32(65535) >= jnp.int32(6554)).astype(jnp.float32)


def layer_norm(columns, norm_gain):
    centre = columns - jnp.mean(columns, axis=0, keepdims=True)
    inverse_dev = lax.rsqrt(jnp.mean(centre * centre, axis=0, keepdims=True) + 1e-06)
    normed = centre * inverse_dev
    return (normed, inverse_dev, (normed * norm_gain[:, None]).astype(jnp.bfloat16))


def norm_back(grad_in, normed, inverse_dev, norm_gain):
    scaled = grad_in * norm_gain[:, None]
    return inverse_dev * (
        scaled
        - jnp.mean(scaled, axis=0, keepdims=True)
        - normed * jnp.mean(scaled * normed, axis=0, keepdims=True)
    )


def gelu_value(pre_act):
    tanh_part = jnp.tanh(gelu_coeff * (pre_act + cubic_coeff * pre_act * pre_act * pre_act))
    return 0.5 * pre_act * (1.0 + tanh_part)


def gelu_slope(pre_act):
    tanh_part = jnp.tanh(gelu_coeff * (pre_act + cubic_coeff * pre_act * pre_act * pre_act))
    return 0.5 * (1.0 + tanh_part) + 0.5 * pre_act * (1.0 - tanh_part * tanh_part) * gelu_coeff * (
        1.0 + 3.0 * cubic_coeff * pre_act * pre_act
    )


def border_lines(grid):
    return jnp.stack([grid[:, 0, :], grid[:, -1, :], grid[:, :, 0], grid[:, :, -1]], axis=0)


def pad_tile(grid, halo):
    zero_corner = jnp.zeros(grid.shape[:1] + (1, 1), grid.dtype)
    middle = jnp.concatenate([halo[2][:, :, None], grid, halo[3][:, :, None]], axis=2)
    top_row = jnp.concatenate([zero_corner, halo[0][:, None, :], zero_corner], axis=2)
    bottom_row = jnp.concatenate([zero_corner, halo[1][:, None, :], zero_corner], axis=2)
    return jnp.concatenate([top_row, middle, bottom_row], axis=1)


def depthwise(padded, depth_kernel):
    side_len = padded.shape[1] - 2
    running = jnp.zeros(padded.shape[:1] + (side_len, side_len), jnp.float32)
    for down_step in range(3):
        for right_step in range(3):
            weight_now = depth_kernel[:, down_step * 3 + right_step][:, None, None]
            running = running + weight_now * padded[
                :, down_step : down_step + side_len, right_step : right_step + side_len
            ].astype(jnp.float32)
    return running


def depth_back(grad_in, depth_kernel):
    side_len = grad_in.shape[1]
    widened = jnp.pad(grad_in, ((0, 0), (2, 2), (2, 2)))
    running = jnp.zeros(grad_in.shape[:1] + (side_len + 2, side_len + 2), jnp.float32)
    for down_step in range(3):
        for right_step in range(3):
            weight_now = depth_kernel[:, down_step * 3 + right_step][:, None, None]
            running = running + weight_now * widened[
                :,
                2 - down_step : 4 - down_step + side_len,
                2 - right_step : 4 - right_step + side_len,
            ]
    return running


def halo_parts(padded):
    return jnp.stack(
        [padded[:, 0, 1:-1], padded[:, -1, 1:-1], padded[:, 1:-1, 0], padded[:, 1:-1, -1]], axis=0
    )


def add_border(interior, border):
    last = interior.shape[1] - 1
    top = jnp.pad(border[0][:, None, :], ((0, 0), (0, last), (0, 0)))
    bottom = jnp.pad(border[1][:, None, :], ((0, 0), (last, 0), (0, 0)))
    left = jnp.pad(border[2][:, :, None], ((0, 0), (0, 0), (0, last)))
    right = jnp.pad(border[3][:, :, None], ((0, 0), (0, 0), (last, 0)))
    return interior + top + bottom + left + right


def shards(
    fields,
    cotangent,
    depth_kernel,
    norm_gain,
    up_weight,
    down_weight,
    layer_scale,
    skip_scale,
    neighbours,
    edge_codes,
    offsets,
    drop_seed,
):
    chan_part, tile_dev, tile_area = fields.shape
    assert tile_dev == 1
    side_len = SIDE
    my_phase = lax.axis_index("sec")
    sections = lax.axis_size("sec")
    ch_index = lax.axis_index("ch")
    ch_count = lax.axis_size("ch")
    tile_count = lax.axis_size("tile")
    my_tile = lax.axis_index("tile")
    hidden = up_weight.shape[2]
    pix_part = tile_area // ch_count

    small = jnp.concatenate([depth_kernel[0].reshape(-1), norm_gain[0], layer_scale[0]])
    small_len = small.shape[0]
    high = lax.reduce_precision(small, exponent_bits=8, mantissa_bits=7)
    rest = small - high
    middle = lax.reduce_precision(rest, exponent_bits=8, mantissa_bits=7)
    low = lax.reduce_precision(rest - middle, exponent_bits=8, mantissa_bits=7)
    parts = jnp.concatenate([high, middle, low]).astype(jnp.bfloat16)
    packed = jnp.concatenate([parts, up_weight[0].reshape(-1), down_weight[0].reshape(-1)])
    packed_got = [packed]
    for shift in range(1, sections):
        route_now = [(i, (i + shift) % sections) for i in range(sections)]
        packed_got.append(lax.ppermute(packed, "sec", route_now))

    def section_weights(s):
        behind = (my_phase - s) % sections
        got = packed_got[0]
        for shift in range(1, sections):
            got = jnp.where(behind == shift, packed_got[shift], got)
        small_s = (
            got[:small_len].astype(jnp.float32) + got[small_len : 2 * small_len].astype(jnp.float32)
        ) + got[2 * small_len : 3 * small_len].astype(jnp.float32)
        large_s = got[3 * small_len :]
        dk_len = chan_part * 9
        cut = up_weight.shape[1] * hidden
        return (
            small_s[:dk_len].reshape(chan_part, 9),
            small_s[dk_len : dk_len + norm_gain.shape[1]],
            small_s[dk_len + norm_gain.shape[1] :],
            large_s[:cut].reshape(up_weight.shape[1:]),
            large_s[cut:].reshape(down_weight.shape[1:]),
        )

    dk_all, gain_all, scale_all, up_all, down_all = [], [], [], [], []
    for s in range(sections):
        for store, part in zip((dk_all, gain_all, scale_all, up_all, down_all), section_weights(s)):
            store.append(part)

    side_code = edge_codes % 4
    own_flip = edge_codes[my_tile] >= 4
    line_ids = jnp.arange(4, dtype=jnp.int32)
    same_tile = neighbours[:, :, None] == neighbours[:, None, :]
    earlier = line_ids[None, :] < line_ids[:, None]
    rank = jnp.sum((same_tile & earlier[None]).astype(jnp.int32), axis=2)
    narrow = jnp.max(rank) < 2

    def send_pick(width):
        hit = (
            (neighbours == my_tile)[:, :, None, None]
            & (rank[:, :, None, None] == jnp.arange(width, dtype=jnp.int32)[None, None, :, None])
            & (side_code[:, :, None, None] == line_ids[None, None, None, :])
        )
        return jnp.sum(hit.astype(jnp.float32), axis=1).astype(jnp.bfloat16)

    def take_pick(width):
        hit = (
            neighbours[my_tile][:, None, None]
            == jnp.arange(tile_count, dtype=jnp.int32)[None, :, None]
        ) & (rank[my_tile][:, None, None] == jnp.arange(width, dtype=jnp.int32)[None, None, :])
        return hit.astype(jnp.bfloat16)

    pixel_ids = offsets[0] + ch_index * pix_part + jnp.arange(pix_part, dtype=jnp.int32)
    unit_ids = jnp.arange(hidden, dtype=jnp.int32)

    def build_send(lines, pick):
        send = jnp.einsum("jrk,kcs->jrcs", pick, lines, preferred_element_type=jnp.float32)
        return send.astype(jnp.bfloat16).reshape(tile_count, -1)

    def receive(send, take, width):
        got = lax.all_to_all(send, "tile", 0, 0, tiled=True)
        got = got.reshape(tile_count, width, chan_part, side_len)
        return jnp.einsum("esr,srcx->ecx", take, got, preferred_element_type=jnp.float32)

    pick_narrow, take_narrow = send_pick(2), take_pick(2)
    pick_wide, take_wide = send_pick(4), take_pick(4)

    def route(lines):
        send_narrow = build_send(lines, pick_narrow)
        return lax.cond(
            narrow,
            lambda sn, ln: receive(sn, take_narrow, 2),
            lambda sn, ln: receive(build_send(ln, pick_wide), take_wide, 4),
            send_narrow,
            lines,
        )

    def to_pixels(block):
        return lax.all_to_all(block, "ch", 1, 0, tiled=True)

    def to_channels(block):
        return lax.all_to_all(block, "ch", 0, 1, tiled=True)

    def block_forward(block_in, s):
        grid = block_in.reshape(chan_part, side_len, side_len)
        halo = route(border_lines(grid)).astype(jnp.bfloat16)
        halo = jnp.where(own_flip[:, None, None], halo[..., ::-1], halo)
        mixed = depthwise(pad_tile(grid, halo), dk_all[s]).astype(jnp.bfloat16)
        mixed = mixed.reshape(chan_part, tile_area)
        if s == 0:
            both = jnp.stack([mixed, last_scaled]).reshape(2, chan_part, ch_count, pix_part)
            both = lax.all_to_all(both, "ch", 2, 1, tiled=True)
            cols = both[0].reshape(-1, pix_part)
            early_cols.append(both[1].reshape(-1, pix_part))
        else:
            cols = to_pixels(mixed)
        normed, inverse_dev, scaled_in = layer_norm(cols.astype(jnp.float32), gain_all[s])
        pre_act = jnp.einsum("ch,cp->hp", up_all[s], scaled_in, preferred_element_type=jnp.float32)
        keeper = keep_mask(drop_seed, s, unit_ids, pixel_ids, hidden)
        dropped = (gelu_value(pre_act) * keeper * drop_scale).astype(jnp.bfloat16)
        branch = jnp.einsum("hc,hp->cp", down_all[s], dropped, preferred_element_type=jnp.float32)
        branch = to_channels(branch)
        out = (
            block_in.astype(jnp.float32) + scale_all[s][:, None] * branch
        ).astype(jnp.bfloat16)
        return out, (normed, inverse_dev, pre_act, keeper)

    def block_backward(grad_out, stored, s):
        normed, inverse_dev, pre_act, keeper = stored
        if s == sections - 1:
            cols = early_cols[0]
        else:
            scaled_grad = (scale_all[s][:, None] * grad_out).astype(jnp.bfloat16)
            cols = to_pixels(scaled_grad)
        grad_drop = jnp.einsum("hc,cp->hp", down_all[s], cols, preferred_element_type=jnp.float32)
        grad_pre = (grad_drop * keeper * drop_scale * gelu_slope(pre_act)).astype(jnp.bfloat16)
        grad_norm = jnp.einsum("ch,hp->cp", up_all[s], grad_pre, preferred_element_type=jnp.float32)
        grad_mixed = norm_back(grad_norm, normed, inverse_dev, gain_all[s])
        grad_mixed = to_channels(grad_mixed).reshape(chan_part, side_len, side_len)
        grad_padded = depth_back(grad_mixed, dk_all[s])
        edge_grad = halo_parts(grad_padded)
        edge_grad = jnp.where(own_flip[:, None, None], edge_grad[..., ::-1], edge_grad).astype(
            jnp.bfloat16
        )
        routed = route(edge_grad)
        interior = add_border(grad_padded[:, 1:-1, 1:-1], routed)
        return grad_out + interior.reshape(chan_part, tile_area)

    skip_col = skip_scale[:, None]
    cot_full = cotangent.reshape(chan_part, tile_area).astype(jnp.float32)
    last_scaled = (scale_all[sections - 1][:, None] * cot_full).astype(jnp.bfloat16)
    early_cols = []
    current = fields.reshape(chan_part, tile_area)
    outs = []
    stores = []
    for s in range(sections):
        if s == sections - 1:
            current = (
                current.astype(jnp.float32) + skip_col * outs[0].astype(jnp.float32)
            ).astype(jnp.bfloat16)
        current, stored = block_forward(current, s)
        outs.append(current)
        stores.append(stored)
    grads = [None] * sections
    grad_now = cot_full
    skip_grad = None
    for s in reversed(range(sections)):
        if s == 0 and sections > 1:
            grad_now = grad_now + skip_grad
        grad_now = block_backward(grad_now, stores[s], s)
        grads[s] = grad_now
        if s == sections - 1:
            skip_grad = skip_col * grad_now
    act_keep = outs[0]
    grad_keep = grads[0]
    for s in range(1, sections):
        act_keep = jnp.where(my_phase == s, outs[s], act_keep)
        grad_keep = jnp.where(my_phase == s, grads[s], grad_keep)
    return (
        act_keep.reshape(1, chan_part, tile_dev, tile_area),
        grad_keep.reshape(1, chan_part, tile_dev, tile_area),
    )


def solution(mesh):
    placed = (
        P("ch", "tile", None),
        P("ch", "tile", None),
        P("sec", "ch", None),
        P("sec", None),
        P("sec", None, None),
        P("sec", None, None),
        P("sec", "ch"),
        P("ch"),
        P(),
        P(),
        P("tile"),
        P(),
    )
    return jax.shard_map(
        shards,
        mesh=mesh,
        in_specs=placed,
        out_specs=(P("sec", "ch", "tile", None), P("sec", "ch", "tile", None)),
        check_vma=False,
    )
```

```python
import jax
import jax.numpy as jnp
from jax import lax
from jax.sharding import PartitionSpec as P

SIDE = 32


drop_scale = 1.0 / 0.9
gelu_coeff = 0.7978845608028654
cubic_coeff = 0.044715


def mix_bits(counter):
    counter = counter * jnp.int32(739982445)
    counter = counter ^ lax.shift_right_logical(counter, jnp.int32(15))
    counter = counter * jnp.int32(695872825)
    counter = counter ^ lax.shift_right_logical(counter, jnp.int32(12))
    return counter


def keep_mask(drop_seed, section, unit_ids, pixels, hidden):
    salted = mix_bits(drop_seed + section * jnp.int32(1000003))
    counter = pixels[None, :] * jnp.int32(hidden) + unit_ids[:, None]
    mixed_bits = mix_bits(counter ^ salted)
    return (mixed_bits & jnp.int32(65535) >= jnp.int32(6554)).astype(jnp.float32)


def layer_norm(columns, norm_gain):
    centre = columns - jnp.mean(columns, axis=0, keepdims=True)
    inverse_dev = lax.rsqrt(jnp.mean(centre * centre, axis=0, keepdims=True) + 1e-06)
    normed = centre * inverse_dev
    return (normed, inverse_dev, (normed * norm_gain[:, None]).astype(jnp.bfloat16))


def norm_back(grad_in, normed, inverse_dev, norm_gain):
    scaled = grad_in * norm_gain[:, None]
    return inverse_dev * (
        scaled
        - jnp.mean(scaled, axis=0, keepdims=True)
        - normed * jnp.mean(scaled * normed, axis=0, keepdims=True)
    )


def gelu_value(pre_act):
    tanh_part = jnp.tanh(gelu_coeff * (pre_act + cubic_coeff * pre_act * pre_act * pre_act))
    return 0.5 * pre_act * (1.0 + tanh_part)


def gelu_slope(pre_act):
    tanh_part = jnp.tanh(gelu_coeff * (pre_act + cubic_coeff * pre_act * pre_act * pre_act))
    return 0.5 * (1.0 + tanh_part) + 0.5 * pre_act * (1.0 - tanh_part * tanh_part) * gelu_coeff * (
        1.0 + 3.0 * cubic_coeff * pre_act * pre_act
    )


def border_lines(grid):
    return jnp.stack([grid[:, 0, :], grid[:, -1, :], grid[:, :, 0], grid[:, :, -1]], axis=0)


def pad_tile(grid, halo):
    zero_corner = jnp.zeros(grid.shape[:1] + (1, 1), grid.dtype)
    middle = jnp.concatenate([halo[2][:, :, None], grid, halo[3][:, :, None]], axis=2)
    top_row = jnp.concatenate([zero_corner, halo[0][:, None, :], zero_corner], axis=2)
    bottom_row = jnp.concatenate([zero_corner, halo[1][:, None, :], zero_corner], axis=2)
    return jnp.concatenate([top_row, middle, bottom_row], axis=1)


def depthwise(padded, depth_kernel):
    side_len = padded.shape[1] - 2
    running = jnp.zeros(padded.shape[:1] + (side_len, side_len), jnp.float32)
    for down_step in range(3):
        for right_step in range(3):
            weight_now = depth_kernel[:, down_step * 3 + right_step][:, None, None]
            running = running + weight_now * padded[
                :, down_step : down_step + side_len, right_step : right_step + side_len
            ].astype(jnp.float32)
    return running


def depth_back(grad_in, depth_kernel):
    side_len = grad_in.shape[1]
    widened = jnp.pad(grad_in, ((0, 0), (2, 2), (2, 2)))
    running = jnp.zeros(grad_in.shape[:1] + (side_len + 2, side_len + 2), jnp.float32)
    for down_step in range(3):
        for right_step in range(3):
            weight_now = depth_kernel[:, down_step * 3 + right_step][:, None, None]
            running = running + weight_now * widened[
                :,
                2 - down_step : 4 - down_step + side_len,
                2 - right_step : 4 - right_step + side_len,
            ]
    return running


def halo_parts(padded):
    return jnp.stack(
        [padded[:, 0, 1:-1], padded[:, -1, 1:-1], padded[:, 1:-1, 0], padded[:, 1:-1, -1]], axis=0
    )


def add_border(interior, border):
    last = interior.shape[1] - 1
    top = jnp.pad(border[0][:, None, :], ((0, 0), (0, last), (0, 0)))
    bottom = jnp.pad(border[1][:, None, :], ((0, 0), (last, 0), (0, 0)))
    left = jnp.pad(border[2][:, :, None], ((0, 0), (0, 0), (0, last)))
    right = jnp.pad(border[3][:, :, None], ((0, 0), (0, 0), (last, 0)))
    return interior + top + bottom + left + right


def shards(*args):
    neighbours = args[8]
    same_tile = neighbours[:, :, None] == neighbours[:, None, :]
    line_ids = jnp.arange(4, dtype=jnp.int32)
    earlier = line_ids[None, :] < line_ids[:, None]
    rank = jnp.sum((same_tile & earlier[None]).astype(jnp.int32), axis=2)
    return lax.cond(
        jnp.max(rank) < 2, lambda *a: whole(2, *a), lambda *a: whole(4, *a), *args
    )


def whole(
    width,
    fields,
    cotangent,
    depth_kernel,
    norm_gain,
    up_weight,
    down_weight,
    layer_scale,
    skip_scale,
    neighbours,
    edge_codes,
    offsets,
    drop_seed,
):
    chan_part, tile_dev, tile_area = fields.shape
    assert tile_dev == 1
    side_len = SIDE
    my_phase = lax.axis_index("sec")
    sections = lax.axis_size("sec")
    ch_index = lax.axis_index("ch")
    ch_count = lax.axis_size("ch")
    tile_count = lax.axis_size("tile")
    my_tile = lax.axis_index("tile")
    hidden = up_weight.shape[2]
    pix_part = tile_area // ch_count

    small = jnp.concatenate([depth_kernel[0].reshape(-1), norm_gain[0], layer_scale[0]])
    small_len = small.shape[0]
    high = lax.reduce_precision(small, exponent_bits=8, mantissa_bits=7)
    rest = small - high
    middle = lax.reduce_precision(rest, exponent_bits=8, mantissa_bits=7)
    low = lax.reduce_precision(rest - middle, exponent_bits=8, mantissa_bits=7)
    parts = jnp.concatenate([high, middle, low]).astype(jnp.bfloat16)
    packed = jnp.concatenate([parts, up_weight[0].reshape(-1), down_weight[0].reshape(-1)])
    packed_got = [packed]
    for shift in range(1, sections):
        route_now = [(i, (i + shift) % sections) for i in range(sections)]
        packed_got.append(lax.ppermute(packed, "sec", route_now))

    def section_weights(s):
        behind = (my_phase - s) % sections
        got = packed_got[0]
        for shift in range(1, sections):
            got = jnp.where(behind == shift, packed_got[shift], got)
        small_s = (
            got[:small_len].astype(jnp.float32) + got[small_len : 2 * small_len].astype(jnp.float32)
        ) + got[2 * small_len : 3 * small_len].astype(jnp.float32)
        large_s = got[3 * small_len :]
        dk_len = chan_part * 9
        cut = up_weight.shape[1] * hidden
        return (
            small_s[:dk_len].reshape(chan_part, 9),
            small_s[dk_len : dk_len + norm_gain.shape[1]],
            small_s[dk_len + norm_gain.shape[1] :],
            large_s[:cut].reshape(up_weight.shape[1:]),
            large_s[cut:].reshape(down_weight.shape[1:]),
        )

    dk_all, gain_all, scale_all, up_all, down_all = [], [], [], [], []
    for s in range(sections):
        for store, part in zip((dk_all, gain_all, scale_all, up_all, down_all), section_weights(s)):
            store.append(part)

    side_code = edge_codes % 4
    own_flip = edge_codes[my_tile] >= 4
    line_ids = jnp.arange(4, dtype=jnp.int32)
    same_tile = neighbours[:, :, None] == neighbours[:, None, :]
    earlier = line_ids[None, :] < line_ids[:, None]
    rank = jnp.sum((same_tile & earlier[None]).astype(jnp.int32), axis=2)

    def send_pick(width):
        hit = (
            (neighbours == my_tile)[:, :, None, None]
            & (rank[:, :, None, None] == jnp.arange(width, dtype=jnp.int32)[None, None, :, None])
            & (side_code[:, :, None, None] == line_ids[None, None, None, :])
        )
        return jnp.sum(hit.astype(jnp.float32), axis=1).astype(jnp.bfloat16)

    def take_pick(width):
        hit = (
            neighbours[my_tile][:, None, None]
            == jnp.arange(tile_count, dtype=jnp.int32)[None, :, None]
        ) & (rank[my_tile][:, None, None] == jnp.arange(width, dtype=jnp.int32)[None, None, :])
        return hit.astype(jnp.bfloat16)

    pixel_ids = offsets[0] + ch_index * pix_part + jnp.arange(pix_part, dtype=jnp.int32)
    unit_ids = jnp.arange(hidden, dtype=jnp.int32)

    def route_with(width):
        pick = send_pick(width)
        take = take_pick(width)

        def run(lines):
            send = jnp.einsum("jrk,kcs->jrcs", pick, lines, preferred_element_type=jnp.float32)
            send = send.astype(jnp.bfloat16).reshape(tile_count, -1)
            got = lax.all_to_all(send, "tile", 0, 0, tiled=True)
            got = got.reshape(tile_count, width, chan_part, side_len)
            return jnp.einsum("esr,srcx->ecx", take, got, preferred_element_type=jnp.float32)

        return run

    route = route_with(width)

    def to_pixels(block):
        return lax.all_to_all(block, "ch", 1, 0, tiled=True)

    def to_channels(block):
        return lax.all_to_all(block, "ch", 0, 1, tiled=True)

    def block_forward(block_in, s):
        grid = block_in.reshape(chan_part, side_len, side_len)
        halo = route(border_lines(grid)).astype(jnp.bfloat16)
        halo = jnp.where(own_flip[:, None, None], halo[..., ::-1], halo)
        mixed = depthwise(pad_tile(grid, halo), dk_all[s]).astype(jnp.bfloat16)
        mixed = mixed.reshape(chan_part, tile_area)
        if s == 0:
            both = jnp.stack([mixed, last_scaled]).reshape(2, chan_part, ch_count, pix_part)
            both = lax.all_to_all(both, "ch", 2, 1, tiled=True)
            cols = both[0].reshape(-1, pix_part)
            early_cols.append(both[1].reshape(-1, pix_part))
        else:
            cols = to_pixels(mixed)
        normed, inverse_dev, scaled_in = layer_norm(cols.astype(jnp.float32), gain_all[s])
        pre_act = jnp.einsum("ch,cp->hp", up_all[s], scaled_in, preferred_element_type=jnp.float32)
        keeper = keep_mask(drop_seed, s, unit_ids, pixel_ids, hidden)
        dropped = (gelu_value(pre_act) * keeper * drop_scale).astype(jnp.bfloat16)
        branch = jnp.einsum("hc,hp->cp", down_all[s], dropped, preferred_element_type=jnp.float32)
        branch = to_channels(branch)
        out = (
            block_in.astype(jnp.float32) + scale_all[s][:, None] * branch
        ).astype(jnp.bfloat16)
        return out, (normed, inverse_dev, pre_act, keeper)

    def block_backward(grad_out, stored, s):
        normed, inverse_dev, pre_act, keeper = stored
        if s == sections - 1:
            cols = early_cols[0]
        else:
            scaled_grad = (scale_all[s][:, None] * grad_out).astype(jnp.bfloat16)
            cols = to_pixels(scaled_grad)
        grad_drop = jnp.einsum("hc,cp->hp", down_all[s], cols, preferred_element_type=jnp.float32)
        grad_pre = (grad_drop * keeper * drop_scale * gelu_slope(pre_act)).astype(jnp.bfloat16)
        grad_norm = jnp.einsum("ch,hp->cp", up_all[s], grad_pre, preferred_element_type=jnp.float32)
        grad_mixed = norm_back(grad_norm, normed, inverse_dev, gain_all[s])
        grad_mixed = to_channels(grad_mixed).reshape(chan_part, side_len, side_len)
        grad_padded = depth_back(grad_mixed, dk_all[s])
        edge_grad = halo_parts(grad_padded)
        edge_grad = jnp.where(own_flip[:, None, None], edge_grad[..., ::-1], edge_grad).astype(
            jnp.bfloat16
        )
        routed = route(edge_grad)
        interior = add_border(grad_padded[:, 1:-1, 1:-1], routed)
        return grad_out + interior.reshape(chan_part, tile_area)

    skip_col = skip_scale[:, None]
    cot_full = cotangent.reshape(chan_part, tile_area).astype(jnp.float32)
    last_scaled = (scale_all[sections - 1][:, None] * cot_full).astype(jnp.bfloat16)
    early_cols = []
    current = fields.reshape(chan_part, tile_area)
    outs = []
    stores = []
    for s in range(sections):
        if s == sections - 1:
            current = (
                current.astype(jnp.float32) + skip_col * outs[0].astype(jnp.float32)
            ).astype(jnp.bfloat16)
        current, stored = block_forward(current, s)
        outs.append(current)
        stores.append(stored)
    grads = [None] * sections
    grad_now = cot_full
    skip_grad = None
    for s in reversed(range(sections)):
        if s == 0 and sections > 1:
            grad_now = grad_now + skip_grad
        grad_now = block_backward(grad_now, stores[s], s)
        grads[s] = grad_now
        if s == sections - 1:
            skip_grad = skip_col * grad_now
    act_keep = outs[0]
    grad_keep = grads[0]
    for s in range(1, sections):
        act_keep = jnp.where(my_phase == s, outs[s], act_keep)
        grad_keep = jnp.where(my_phase == s, grads[s], grad_keep)
    return (
        act_keep.reshape(1, chan_part, tile_dev, tile_area),
        grad_keep.reshape(1, chan_part, tile_dev, tile_area),
    )


def solution(mesh):
    placed = (
        P("ch", "tile", None),
        P("ch", "tile", None),
        P("sec", "ch", None),
        P("sec", None),
        P("sec", None, None),
        P("sec", None, None),
        P("sec", "ch"),
        P("ch"),
        P(),
        P(),
        P("tile"),
        P(),
    )
    return jax.shard_map(
        shards,
        mesh=mesh,
        in_specs=placed,
        out_specs=(P("sec", "ch", "tile", None), P("sec", "ch", "tile", None)),
        check_vma=False,
    )
```

```python
import jax
import jax.numpy as jnp
from jax import lax
from jax.sharding import PartitionSpec as P

SIDE = 32


drop_scale = 1.0 / 0.9
gelu_coeff = 0.7978845608028654
cubic_coeff = 0.044715


def mix_bits(counter):
    counter = counter * jnp.int32(739982445)
    counter = counter ^ lax.shift_right_logical(counter, jnp.int32(15))
    counter = counter * jnp.int32(695872825)
    counter = counter ^ lax.shift_right_logical(counter, jnp.int32(12))
    return counter


def keep_mask(drop_seed, section, unit_ids, pixels, hidden):
    salted = mix_bits(drop_seed + section * jnp.int32(1000003))
    counter = pixels[None, :] * jnp.int32(hidden) + unit_ids[:, None]
    mixed_bits = mix_bits(counter ^ salted)
    return (mixed_bits & jnp.int32(65535) >= jnp.int32(6554)).astype(jnp.float32)


def layer_norm(columns, norm_gain):
    centre = columns - jnp.mean(columns, axis=0, keepdims=True)
    inverse_dev = lax.rsqrt(jnp.mean(centre * centre, axis=0, keepdims=True) + 1e-06)
    normed = centre * inverse_dev
    return (normed, inverse_dev, (normed * norm_gain[:, None]).astype(jnp.bfloat16))


def norm_back(grad_in, normed, inverse_dev, norm_gain):
    scaled = grad_in * norm_gain[:, None]
    return inverse_dev * (
        scaled
        - jnp.mean(scaled, axis=0, keepdims=True)
        - normed * jnp.mean(scaled * normed, axis=0, keepdims=True)
    )


def gelu_value(pre_act):
    tanh_part = jnp.tanh(gelu_coeff * (pre_act + cubic_coeff * pre_act * pre_act * pre_act))
    return 0.5 * pre_act * (1.0 + tanh_part)


def gelu_slope(pre_act):
    tanh_part = jnp.tanh(gelu_coeff * (pre_act + cubic_coeff * pre_act * pre_act * pre_act))
    return 0.5 * (1.0 + tanh_part) + 0.5 * pre_act * (1.0 - tanh_part * tanh_part) * gelu_coeff * (
        1.0 + 3.0 * cubic_coeff * pre_act * pre_act
    )


def border_lines(grid):
    return jnp.stack([grid[:, 0, :], grid[:, -1, :], grid[:, :, 0], grid[:, :, -1]], axis=0)


def pad_tile(grid, halo):
    zero_corner = jnp.zeros(grid.shape[:1] + (1, 1), grid.dtype)
    middle = jnp.concatenate([halo[2][:, :, None], grid, halo[3][:, :, None]], axis=2)
    top_row = jnp.concatenate([zero_corner, halo[0][:, None, :], zero_corner], axis=2)
    bottom_row = jnp.concatenate([zero_corner, halo[1][:, None, :], zero_corner], axis=2)
    return jnp.concatenate([top_row, middle, bottom_row], axis=1)


def depthwise(padded, depth_kernel):
    side_len = padded.shape[1] - 2
    running = jnp.zeros(padded.shape[:1] + (side_len, side_len), jnp.float32)
    for down_step in range(3):
        for right_step in range(3):
            weight_now = depth_kernel[:, down_step * 3 + right_step][:, None, None]
            running = running + weight_now * padded[
                :, down_step : down_step + side_len, right_step : right_step + side_len
            ].astype(jnp.float32)
    return running


def depth_back(grad_in, depth_kernel):
    side_len = grad_in.shape[1]
    widened = jnp.pad(grad_in, ((0, 0), (2, 2), (2, 2)))
    running = jnp.zeros(grad_in.shape[:1] + (side_len + 2, side_len + 2), jnp.float32)
    for down_step in range(3):
        for right_step in range(3):
            weight_now = depth_kernel[:, down_step * 3 + right_step][:, None, None]
            running = running + weight_now * widened[
                :,
                2 - down_step : 4 - down_step + side_len,
                2 - right_step : 4 - right_step + side_len,
            ]
    return running


def halo_parts(padded):
    return jnp.stack(
        [padded[:, 0, 1:-1], padded[:, -1, 1:-1], padded[:, 1:-1, 0], padded[:, 1:-1, -1]], axis=0
    )


def add_border(interior, border):
    last = interior.shape[1] - 1
    top = jnp.pad(border[0][:, None, :], ((0, 0), (0, last), (0, 0)))
    bottom = jnp.pad(border[1][:, None, :], ((0, 0), (last, 0), (0, 0)))
    left = jnp.pad(border[2][:, :, None], ((0, 0), (0, 0), (0, last)))
    right = jnp.pad(border[3][:, :, None], ((0, 0), (0, 0), (last, 0)))
    return interior + top + bottom + left + right


def shards(*args):
    neighbours = args[8]
    same_tile = neighbours[:, :, None] == neighbours[:, None, :]
    line_ids = jnp.arange(4, dtype=jnp.int32)
    earlier = line_ids[None, :] < line_ids[:, None]
    rank = jnp.sum((same_tile & earlier[None]).astype(jnp.int32), axis=2)
    packed_got = send_weights(*args[2:7])
    return lax.cond(
        jnp.max(rank) < 2,
        lambda *a: whole(2, *a),
        lambda *a: whole(4, *a),
        *(args + tuple(packed_got)),
    )


def send_weights(depth_kernel, norm_gain, up_weight, down_weight, layer_scale):
    sections = lax.axis_size("sec")
    small = jnp.concatenate([depth_kernel[0].reshape(-1), norm_gain[0], layer_scale[0]])
    high = lax.reduce_precision(small, exponent_bits=8, mantissa_bits=7)
    rest = small - high
    middle = lax.reduce_precision(rest, exponent_bits=8, mantissa_bits=7)
    low = lax.reduce_precision(rest - middle, exponent_bits=8, mantissa_bits=7)
    parts = jnp.concatenate([high, middle, low]).astype(jnp.bfloat16)
    packed = jnp.concatenate([parts, up_weight[0].reshape(-1), down_weight[0].reshape(-1)])
    packed_got = [packed]
    for shift in range(1, sections):
        route_now = [(i, (i + shift) % sections) for i in range(sections)]
        packed_got.append(lax.ppermute(packed, "sec", route_now))

    return packed_got


def whole(
    width,
    fields,
    cotangent,
    depth_kernel,
    norm_gain,
    up_weight,
    down_weight,
    layer_scale,
    skip_scale,
    neighbours,
    edge_codes,
    offsets,
    drop_seed,
    *packed_got,
):
    chan_part, tile_dev, tile_area = fields.shape
    small_len = chan_part * 9 + norm_gain.shape[1] + layer_scale.shape[1]
    assert tile_dev == 1
    side_len = SIDE
    my_phase = lax.axis_index("sec")
    sections = lax.axis_size("sec")
    ch_index = lax.axis_index("ch")
    ch_count = lax.axis_size("ch")
    tile_count = lax.axis_size("tile")
    my_tile = lax.axis_index("tile")
    hidden = up_weight.shape[2]
    pix_part = tile_area // ch_count

    def section_weights(s):
        behind = (my_phase - s) % sections
        got = packed_got[0]
        for shift in range(1, sections):
            got = jnp.where(behind == shift, packed_got[shift], got)
        small_s = (
            got[:small_len].astype(jnp.float32) + got[small_len : 2 * small_len].astype(jnp.float32)
        ) + got[2 * small_len : 3 * small_len].astype(jnp.float32)
        large_s = got[3 * small_len :]
        dk_len = chan_part * 9
        cut = up_weight.shape[1] * hidden
        return (
            small_s[:dk_len].reshape(chan_part, 9),
            small_s[dk_len : dk_len + norm_gain.shape[1]],
            small_s[dk_len + norm_gain.shape[1] :],
            large_s[:cut].reshape(up_weight.shape[1:]),
            large_s[cut:].reshape(down_weight.shape[1:]),
        )

    dk_all, gain_all, scale_all, up_all, down_all = [], [], [], [], []
    for s in range(sections):
        for store, part in zip((dk_all, gain_all, scale_all, up_all, down_all), section_weights(s)):
            store.append(part)

    side_code = edge_codes % 4
    own_flip = edge_codes[my_tile] >= 4
    line_ids = jnp.arange(4, dtype=jnp.int32)
    same_tile = neighbours[:, :, None] == neighbours[:, None, :]
    earlier = line_ids[None, :] < line_ids[:, None]
    rank = jnp.sum((same_tile & earlier[None]).astype(jnp.int32), axis=2)

    def send_pick(width):
        hit = (
            (neighbours == my_tile)[:, :, None, None]
            & (rank[:, :, None, None] == jnp.arange(width, dtype=jnp.int32)[None, None, :, None])
            & (side_code[:, :, None, None] == line_ids[None, None, None, :])
        )
        return jnp.sum(hit.astype(jnp.float32), axis=1).astype(jnp.bfloat16)

    def take_pick(width):
        hit = (
            neighbours[my_tile][:, None, None]
            == jnp.arange(tile_count, dtype=jnp.int32)[None, :, None]
        ) & (rank[my_tile][:, None, None] == jnp.arange(width, dtype=jnp.int32)[None, None, :])
        return hit.astype(jnp.bfloat16)

    pixel_ids = offsets[0] + ch_index * pix_part + jnp.arange(pix_part, dtype=jnp.int32)
    unit_ids = jnp.arange(hidden, dtype=jnp.int32)

    def route_with(width):
        pick = send_pick(width)
        take = take_pick(width)

        def run(lines):
            send = jnp.einsum("jrk,kcs->jrcs", pick, lines, preferred_element_type=jnp.float32)
            send = send.astype(jnp.bfloat16).reshape(tile_count, -1)
            got = lax.all_to_all(send, "tile", 0, 0, tiled=True)
            got = got.reshape(tile_count, width, chan_part, side_len)
            return jnp.einsum("esr,srcx->ecx", take, got, preferred_element_type=jnp.float32)

        return run

    route = route_with(width)

    def to_pixels(block):
        return lax.all_to_all(block, "ch", 1, 0, tiled=True)

    def to_channels(block):
        return lax.all_to_all(block, "ch", 0, 1, tiled=True)

    def block_forward(block_in, s):
        grid = block_in.reshape(chan_part, side_len, side_len)
        halo = route(border_lines(grid)).astype(jnp.bfloat16)
        halo = jnp.where(own_flip[:, None, None], halo[..., ::-1], halo)
        mixed = depthwise(pad_tile(grid, halo), dk_all[s]).astype(jnp.bfloat16)
        mixed = mixed.reshape(chan_part, tile_area)
        if s == 0:
            both = jnp.stack([mixed, last_scaled]).reshape(2, chan_part, ch_count, pix_part)
            both = lax.all_to_all(both, "ch", 2, 1, tiled=True)
            cols = both[0].reshape(-1, pix_part)
            early_cols.append(both[1].reshape(-1, pix_part))
        else:
            cols = to_pixels(mixed)
        normed, inverse_dev, scaled_in = layer_norm(cols.astype(jnp.float32), gain_all[s])
        pre_act = jnp.einsum("ch,cp->hp", up_all[s], scaled_in, preferred_element_type=jnp.float32)
        keeper = keep_mask(drop_seed, s, unit_ids, pixel_ids, hidden)
        dropped = (gelu_value(pre_act) * keeper * drop_scale).astype(jnp.bfloat16)
        branch = jnp.einsum("hc,hp->cp", down_all[s], dropped, preferred_element_type=jnp.float32)
        branch = to_channels(branch)
        out = (
            block_in.astype(jnp.float32) + scale_all[s][:, None] * branch
        ).astype(jnp.bfloat16)
        return out, (normed, inverse_dev, pre_act, keeper)

    def block_backward(grad_out, stored, s):
        normed, inverse_dev, pre_act, keeper = stored
        if s == sections - 1:
            cols = early_cols[0]
        else:
            scaled_grad = (scale_all[s][:, None] * grad_out).astype(jnp.bfloat16)
            cols = to_pixels(scaled_grad)
        grad_drop = jnp.einsum("hc,cp->hp", down_all[s], cols, preferred_element_type=jnp.float32)
        grad_pre = (grad_drop * keeper * drop_scale * gelu_slope(pre_act)).astype(jnp.bfloat16)
        grad_norm = jnp.einsum("ch,hp->cp", up_all[s], grad_pre, preferred_element_type=jnp.float32)
        grad_mixed = norm_back(grad_norm, normed, inverse_dev, gain_all[s])
        grad_mixed = to_channels(grad_mixed).reshape(chan_part, side_len, side_len)
        grad_padded = depth_back(grad_mixed, dk_all[s])
        edge_grad = halo_parts(grad_padded)
        edge_grad = jnp.where(own_flip[:, None, None], edge_grad[..., ::-1], edge_grad).astype(
            jnp.bfloat16
        )
        routed = route(edge_grad)
        interior = add_border(grad_padded[:, 1:-1, 1:-1], routed)
        return grad_out + interior.reshape(chan_part, tile_area)

    skip_col = skip_scale[:, None]
    cot_full = cotangent.reshape(chan_part, tile_area).astype(jnp.float32)
    last_scaled = (scale_all[sections - 1][:, None] * cot_full).astype(jnp.bfloat16)
    early_cols = []
    current = fields.reshape(chan_part, tile_area)
    outs = []
    stores = []
    for s in range(sections):
        if s == sections - 1:
            current = (
                current.astype(jnp.float32) + skip_col * outs[0].astype(jnp.float32)
            ).astype(jnp.bfloat16)
        current, stored = block_forward(current, s)
        outs.append(current)
        stores.append(stored)
    grads = [None] * sections
    grad_now = cot_full
    skip_grad = None
    for s in reversed(range(sections)):
        if s == 0 and sections > 1:
            grad_now = grad_now + skip_grad
        grad_now = block_backward(grad_now, stores[s], s)
        grads[s] = grad_now
        if s == sections - 1:
            skip_grad = skip_col * grad_now
    act_keep = outs[0]
    grad_keep = grads[0]
    for s in range(1, sections):
        act_keep = jnp.where(my_phase == s, outs[s], act_keep)
        grad_keep = jnp.where(my_phase == s, grads[s], grad_keep)
    return (
        act_keep.reshape(1, chan_part, tile_dev, tile_area),
        grad_keep.reshape(1, chan_part, tile_dev, tile_area),
    )


def solution(mesh):
    placed = (
        P("ch", "tile", None),
        P("ch", "tile", None),
        P("sec", "ch", None),
        P("sec", None),
        P("sec", None, None),
        P("sec", None, None),
        P("sec", "ch"),
        P("ch"),
        P(),
        P(),
        P("tile"),
        P(),
    )
    return jax.shard_map(
        shards,
        mesh=mesh,
        in_specs=placed,
        out_specs=(P("sec", "ch", "tile", None), P("sec", "ch", "tile", None)),
        check_vma=False,
    )
```
